256 devices in a mesh: region: 8 (over z), rows: 32 (over y, x, core).
Axes of the slice: x: 4, y: 4, z: 8, core: 2. Of those that a mesh axis runs over, the one named last changes fastest.
Arguments:
- ensemble_state: float32 [524288, 256], P(('region', 'rows')), may hold values from -16 to 16
- obs_values: float32 [4, 1024], replicated, may hold values from -16 to 16
- obs_error: float32 [4, 1024], replicated, may hold values from 0.1 to 2
- batch_owner: int32 [4], replicated, may hold values from 0 to 7
- readers: int32 [4, 3], replicated, may hold values from 0 to 7
- obs_order: int32 [4, 1024], replicated, may hold values from 0 to 1023, each once within a row
- obs_rows: int32 [4, 1024], replicated, may hold values from 0 to 2047
- loc_taper: float32 [4, 8, 1024], replicated, may hold values from 0.02 to 0.3
Outputs:
- analysis: float32 [524288, 256], P(('region', 'rows'))
The draws below stay inside these ranges and needn't reach their ends.
Inputs may be any that keep to these rules, and one draw needn't show every extreme that they name: Each row of obs_order holds every observation number once. `readers`: regions that read a batch besides its owner region; repeats allowed.
All inputs are finite; a program needn't handle non-finite values.
Results may differ from the reference program's by a relative error of at most 0.0024.
Values may be sent and summed in bfloat16 or wider, within the bound.
No kernel may reach another device: no remote copies, remote signals or barrier semaphores. Data moves between devices by JAX's collectives and lax.ppermute only.
A program may use at most 64 MiB of HBM per device.

```python
import math
import jax
import jax.numpy as jnp
from jax import lax

MEMBERS = 256
OBS = 1024
BATCHES = 4
READERS = 3
ROWS_DEV = 2048
REGIONS = 8
GROUP = 32
SLOTS = 32
STATE_ROWS = 524288


def draw_ensemble_state(key, part):
    key_centre, key_spread, key_noise = jax.random.split(key, 3)
    centre = jax.random.uniform(key_centre, (STATE_ROWS, 1), jnp.float32, -8.0, 8.0)
    spread = jnp.exp(jax.random.uniform(key_spread, (STATE_ROWS, 1), jnp.float32, math.log(0.2), math.log(2.0)))
    noise_part = jnp.clip(jax.random.normal(key_noise, (STATE_ROWS, MEMBERS), jnp.float32), -3.5, 3.5)
    return centre + spread * noise_part


def plant(array, key, low, high):
    index_at = [jax.random.randint(jax.random.fold_in(key, axis), (), 0, length) for axis, length in enumerate(array.shape)]
    main_axis = array.shape.index(max(array.shape))
    beside = index_at[:main_axis] + [(index_at[main_axis] + 1) % array.shape[main_axis]] + index_at[main_axis + 1:]
    return array.at[tuple(index_at)].set(low).at[tuple(beside)].set(high)


def centred(own_key, dims, scale, bound, kind=jnp.bfloat16):
    result = jax.random.normal(own_key, dims, jnp.float32) * scale
    return jnp.minimum(jnp.maximum(result, -bound), bound).astype(kind)


def setup_inputs(seed: int = 0) -> dict:
    streams_of = jax.random.split(jax.random.key(seed), 9)
    ensemble_state = draw_ensemble_state(jax.random.fold_in(streams_of[8], 71), 0)
    obs_values = centred(streams_of[1], (BATCHES, OBS), 3.0, 16.0, jnp.float32)
    obs_error = jnp.clip(jnp.exp(jax.random.uniform(streams_of[2], (BATCHES, OBS), jnp.float32, math.log(0.1), math.log(2.0))), 0.1, 2.0)
    batch_owner = plant(jax.random.randint(streams_of[3], (BATCHES,), 0, REGIONS), jax.random.fold_in(streams_of[3], 1), 0, REGIONS - 1).astype(jnp.int32)
    readers = plant(jax.random.randint(streams_of[4], (BATCHES, READERS), 0, REGIONS), jax.random.fold_in(streams_of[4], 1), 0, REGIONS - 1).astype(jnp.int32)
    obs_order = jax.vmap(lambda own: jax.random.permutation(own, OBS))(jax.random.split(streams_of[5], BATCHES)).reshape((BATCHES, OBS)).astype(jnp.int32)
    obs_rows = plant(jax.random.randint(streams_of[6], (BATCHES, OBS), 0, ROWS_DEV), jax.random.fold_in(streams_of[6], 1), 0, ROWS_DEV - 1).astype(jnp.int32)
    loc_taper = jnp.clip(jnp.exp(jax.random.uniform(streams_of[7], (BATCHES, REGIONS, OBS), jnp.float32, math.log(0.02), math.log(0.3))), 0.02, 0.3)
    return dict(ensemble_state=ensemble_state, obs_values=obs_values, obs_error=obs_error, batch_owner=batch_owner, readers=readers, obs_order=obs_order, obs_rows=obs_rows, loc_taper=loc_taper)


def adjust(prior_ens, values, errors):
    members = prior_ens.shape[1]
    prior_mean = lax.optimization_barrier(jnp.mean(prior_ens, axis=1, keepdims=True))
    anomalies = prior_ens - prior_mean
    variance = lax.optimization_barrier(jnp.sum(anomalies * anomalies, axis=1, keepdims=True)) / (members - 1) + 1e-05
    errors = errors[:, None]
    values = values[:, None]
    post_var = variance * errors / (variance + errors)
    mean_shift = post_var * (prior_mean / variance + values / errors) - prior_mean
    shrink = jnp.sqrt(errors / (variance + errors))
    obs_incr = (mean_shift + (shrink - 1.0) * anomalies).astype(jnp.bfloat16)
    scaled = (anomalies / ((members - 1) * variance)).astype(jnp.bfloat16)
    return (scaled, obs_incr)

def update_block(block_x, scaled, obs_incr, weights):
    centre = lax.optimization_barrier(jnp.mean(block_x, axis=1, keepdims=True))
    state_anom = (block_x - centre).astype(jnp.bfloat16)
    linked = lax.dot_general(state_anom, scaled, (((1,), (1,)), ((), ())), preferred_element_type=jnp.float32)
    coupling = (linked * weights[None, :]).astype(jnp.bfloat16)
    return block_x + jnp.dot(coupling, obs_incr, preferred_element_type=jnp.float32)

def reference(ensemble_state, obs_values, obs_error, batch_owner, readers, obs_order, obs_rows, loc_taper):
    members = ensemble_state.shape[1]
    blocks = ensemble_state.reshape(REGIONS * GROUP, ROWS_DEV, members)
    block_region = (jnp.arange(REGIONS * GROUP) // GROUP).astype(jnp.int32)
    slot_column = (jnp.arange(OBS) // SLOTS).astype(jnp.int32)
    region_ids = jnp.arange(REGIONS).astype(jnp.int32)
    for batch_idx in range(BATCHES):
        source = (batch_owner[batch_idx] * GROUP + slot_column).astype(jnp.int32)
        picked = blocks[source, obs_rows[batch_idx]]
        prior_ens = jnp.zeros((OBS, members), jnp.float32).at[obs_order[batch_idx]].set(picked)
        scaled, obs_incr = adjust(prior_ens, obs_values[batch_idx], obs_error[batch_idx])
        reads_mask = jnp.logical_or(region_ids == batch_owner[batch_idx], jnp.any(readers[batch_idx][None, :] == region_ids[:, None], axis=1))
        tapers = loc_taper[batch_idx]

        def advance(entry_pair, scaled=scaled, obs_incr=obs_incr, reads_mask=reads_mask, tapers=tapers):
            block_x, region = entry_pair
            return lax.cond(reads_mask[region], lambda rows_x: update_block(rows_x, scaled, obs_incr, tapers[region]), lambda rows_x: rows_x, block_x)
        blocks = lax.map(advance, (blocks, block_region))
    return blocks.reshape(STATE_ROWS, members)
```

```python
import jax
import jax.numpy as jnp
from jax import lax
from jax.sharding import PartitionSpec as P


def adjust(prior_ens, values, errors):
    members = prior_ens.shape[1]
    prior_mean = jnp.mean(prior_ens, axis=1, keepdims=True)
    anomalies = prior_ens - prior_mean
    variance = jnp.sum(anomalies * anomalies, axis=1, keepdims=True) / (members - 1) + 1e-05
    errors = errors[:, None]
    values = values[:, None]
    post_var = variance * errors / (variance + errors)
    mean_shift = post_var * (prior_mean / variance + values / errors) - prior_mean
    shrink = jnp.sqrt(errors / (variance + errors))
    obs_incr = (mean_shift + (shrink - 1.0) * anomalies).astype(jnp.bfloat16)
    scaled = (anomalies / ((members - 1) * variance)).astype(jnp.bfloat16)
    return (scaled, obs_incr)


def update_block(block_x, scaled, obs_incr, weights):
    centre = jnp.mean(block_x, axis=1, keepdims=True)
    state_anom = (block_x - centre).astype(jnp.bfloat16)
    linked = lax.dot_general(
        state_anom, scaled, (((1,), (1,)), ((), ())), preferred_element_type=jnp.float32
    )
    coupling = (linked * weights[None, :]).astype(jnp.bfloat16)
    return block_x + jnp.dot(coupling, obs_incr, preferred_element_type=jnp.float32)


def pick_owner(pieces, owners, axis):
    size = lax.axis_size(axis)
    me = lax.axis_index(axis)
    held = pieces
    step = 1
    while step < size:
        partner = lax.ppermute(held, axis, [(i, i ^ step) for i in range(size)])
        keep = ((me // step) % 2) == ((owners // step) % 2)
        held = jnp.where(keep[:, None, None], held, partner)
        step *= 2
    return held


def local(
    ensemble_state, obs_values, obs_error, batch_owner, readers, obs_order, obs_rows, loc_taper
):
    group_size = lax.axis_size("rows")
    region_count = lax.axis_size("region")
    region_idx = lax.axis_index("region")
    column_idx = lax.axis_index("rows")
    batches, obs_count = obs_order.shape
    slot_count = obs_count // group_size
    members = ensemble_state.shape[1]

    own_rows = lax.dynamic_slice_in_dim(obs_rows, column_idx * slot_count, slot_count, axis=1)
    pieces = ensemble_state[own_rows]
    pieces = pick_owner(pieces, batch_owner, "region")
    raw = lax.all_gather(pieces, "rows", axis=1, tiled=True)

    region_ids = jnp.arange(region_count, dtype=jnp.int32)
    reads = jnp.logical_or(
        region_ids[None, :] == batch_owner[:, None],
        jnp.any(readers[:, :, None] == region_ids[None, None, :], axis=1),
    )
    slot_taper = jnp.take_along_axis(loc_taper, obs_order[:, None, :], axis=2)
    slot_values = jnp.take_along_axis(obs_values, obs_order, axis=1)
    slot_errors = jnp.take_along_axis(obs_error, obs_order, axis=1)

    adjusted = []
    for batch_idx in range(batches):
        prior = raw[batch_idx]
        owner = batch_owner[batch_idx]
        for earlier in range(batch_idx):
            scaled, obs_incr = adjusted[earlier]
            weights = slot_taper[earlier, owner]
            prior = lax.cond(
                reads[earlier, owner],
                lambda rows_x, s=scaled, o=obs_incr, w=weights: update_block(rows_x, s, o, w),
                lambda rows_x: rows_x,
                prior,
            )
        adjusted.append(adjust(prior, slot_values[batch_idx], slot_errors[batch_idx]))

    current = ensemble_state
    for batch_idx in range(batches):
        scaled, obs_incr = adjusted[batch_idx]
        weights = slot_taper[batch_idx, region_idx]
        current = lax.cond(
            reads[batch_idx, region_idx],
            lambda rows_x, s=scaled, o=obs_incr, w=weights: update_block(rows_x, s, o, w),
            lambda rows_x: rows_x,
            current,
        )
    return current


def solution(mesh):
    placed = (P(("region", "rows"), None), P(), P(), P(), P(), P(), P(), P())
    return jax.shard_map(
        local, mesh=mesh, in_specs=placed, out_specs=P(("region", "rows"), None), check_vma=False
    )
```

```python
import jax
import jax.numpy as jnp
from jax import lax
from jax.sharding import PartitionSpec as P


def adjust(prior_ens, values, errors):
    members = prior_ens.shape[1]
    prior_mean = jnp.mean(prior_ens, axis=1, keepdims=True)
    anomalies = prior_ens - prior_mean
    variance = jnp.sum(anomalies * anomalies, axis=1, keepdims=True) / (members - 1) + 1e-05
    errors = errors[:, None]
    values = values[:, None]
    post_var = variance * errors / (variance + errors)
    mean_shift = post_var * (prior_mean / variance + values / errors) - prior_mean
    shrink = jnp.sqrt(errors / (variance + errors))
    obs_incr = (mean_shift + (shrink - 1.0) * anomalies).astype(jnp.bfloat16)
    scaled = (anomalies / ((members - 1) * variance)).astype(jnp.bfloat16)
    return (scaled, obs_incr)


def update_block(block_x, scaled, obs_incr, weights):
    centre = jnp.mean(block_x, axis=1, keepdims=True)
    state_anom = (block_x - centre).astype(jnp.bfloat16)
    linked = lax.dot_general(
        state_anom, scaled, (((1,), (1,)), ((), ())), preferred_element_type=jnp.float32
    )
    coupling = (linked * weights[None, :]).astype(jnp.bfloat16)
    return block_x + jnp.dot(coupling, obs_incr, preferred_element_type=jnp.float32)


def pick_owner(pieces, owners, axis):
    size = lax.axis_size(axis)
    me = lax.axis_index(axis)
    held = pieces
    step = 1
    while step < size:
        partner = lax.ppermute(held, axis, [(i, i ^ step) for i in range(size)])
        keep = ((me // step) % 2) == ((owners // step) % 2)
        held = jnp.where(keep[:, None, None], held, partner)
        step *= 2
    return held


def local(
    ensemble_state, obs_values, obs_error, batch_owner, readers, obs_order, obs_rows, loc_taper
):
    group_size = lax.axis_size("rows")
    region_count = lax.axis_size("region")
    region_idx = lax.axis_index("region")
    column_idx = lax.axis_index("rows")
    batches, obs_count = obs_order.shape
    slot_count = obs_count // group_size
    members = ensemble_state.shape[1]

    own_rows = lax.dynamic_slice_in_dim(obs_rows, column_idx * slot_count, slot_count, axis=1)
    pieces = ensemble_state[own_rows]
    pieces = pick_owner(pieces, batch_owner, "region")
    raw = lax.all_gather(pieces, "rows", axis=1, tiled=True)

    region_ids = jnp.arange(region_count, dtype=jnp.int32)
    reads = jnp.logical_or(
        region_ids[None, :] == batch_owner[:, None],
        jnp.any(readers[:, :, None] == region_ids[None, None, :], axis=1),
    )
    priors = jnp.zeros((batches, obs_count, members), jnp.float32)
    priors = jax.vmap(lambda empty, order, rows: empty.at[order].set(rows))(priors, obs_order, raw)
    owner_reads = jnp.take_along_axis(reads, jnp.broadcast_to(batch_owner[None, :], (batches, batches)), axis=1)

    def chain_step(earlier, carry):
        priors, scaled_all, incr_all = carry
        scaled, obs_incr = adjust(priors[earlier], obs_values[earlier], obs_error[earlier])
        scaled_all = lax.dynamic_update_index_in_dim(scaled_all, scaled, earlier, 0)
        incr_all = lax.dynamic_update_index_in_dim(incr_all, obs_incr, earlier, 0)

        def later_step(later, priors):
            weights = loc_taper[earlier, batch_owner[later]]
            updated = lax.cond(
                jnp.logical_and(later > earlier, owner_reads[earlier, later]),
                lambda rows_x: update_block(rows_x, scaled, obs_incr, weights),
                lambda rows_x: rows_x,
                priors[later],
            )
            return lax.dynamic_update_index_in_dim(priors, updated, later, 0)

        priors = lax.fori_loop(earlier + 1, batches, later_step, priors)
        return priors, scaled_all, incr_all

    empty = jnp.zeros((batches, obs_count, members), jnp.bfloat16)
    _, scaled_all, incr_all = lax.fori_loop(0, batches, chain_step, (priors, empty, empty))

    def main_step(batch_idx, current):
        weights = loc_taper[batch_idx, region_idx]
        return lax.cond(
            reads[batch_idx, region_idx],
            lambda rows_x: update_block(rows_x, scaled_all[batch_idx], incr_all[batch_idx], weights),
            lambda rows_x: rows_x,
            current,
        )

    current = lax.fori_loop(0, batches, main_step, ensemble_state)
    return current


def solution(mesh):
    placed = (P(("region", "rows"), None), P(), P(), P(), P(), P(), P(), P())
    return jax.shard_map(
        local, mesh=mesh, in_specs=placed, out_specs=P(("region", "rows"), None), check_vma=False
    )
```

```python
import jax
import jax.numpy as jnp
from jax import lax
from jax.experimental import pallas as pl
from jax.sharding import PartitionSpec as P


def adjust(prior_ens, values, errors):
    members = prior_ens.shape[1]
    prior_mean = jnp.mean(prior_ens, axis=1, keepdims=True)
    anomalies = prior_ens - prior_mean
    variance = jnp.sum(anomalies * anomalies, axis=1, keepdims=True) / (members - 1) + 1e-05
    errors = errors[:, None]
    values = values[:, None]
    post_var = variance * errors / (variance + errors)
    mean_shift = post_var * (prior_mean / variance + values / errors) - prior_mean
    shrink = jnp.sqrt(errors / (variance + errors))
    obs_incr = (mean_shift + (shrink - 1.0) * anomalies).astype(jnp.bfloat16)
    scaled = (anomalies / ((members - 1) * variance)).astype(jnp.bfloat16)
    return (scaled, obs_incr)


def adjust_kernel(prior_ref, values_ref, errors_ref, scaled_ref, incr_ref):
    scaled, obs_incr = adjust(prior_ref[...], values_ref[...][:, 0], errors_ref[...][:, 0])
    scaled_ref[...] = scaled
    incr_ref[...] = obs_incr


def adjust_rows(prior, values, errors, block=256):
    rows, members = prior.shape
    row_spec = pl.BlockSpec((block, members), lambda i: (i, 0))
    col_spec = pl.BlockSpec((block, 1), lambda i: (i, 0))
    out = jax.ShapeDtypeStruct((rows, members), jnp.bfloat16)
    return pl.pallas_call(
        adjust_kernel,
        grid=(rows // block,),
        in_specs=[row_spec, col_spec, col_spec],
        out_specs=[row_spec, row_spec],
        out_shape=[out, out],
    )(prior, values[:, None], errors[:, None])


def update_block(block_x, scaled, obs_incr, weights):
    centre = jnp.mean(block_x, axis=1, keepdims=True)
    state_anom = (block_x - centre).astype(jnp.bfloat16)
    linked = lax.dot_general(
        state_anom, scaled, (((1,), (1,)), ((), ())), preferred_element_type=jnp.float32
    )
    coupling = (linked * weights[None, :]).astype(jnp.bfloat16)
    return block_x + jnp.dot(coupling, obs_incr, preferred_element_type=jnp.float32)


def pick_owner(pieces, owners, axis):
    size = lax.axis_size(axis)
    me = lax.axis_index(axis)
    held = pieces
    step = 1
    while step < size:
        partner = lax.ppermute(held, axis, [(i, i ^ step) for i in range(size)])
        keep = ((me // step) % 2) == ((owners // step) % 2)
        held = jnp.where(keep[:, None, None], held, partner)
        step *= 2
    return held


def local(
    ensemble_state, obs_values, obs_error, batch_owner, readers, obs_order, obs_rows, loc_taper
):
    group_size = lax.axis_size("rows")
    region_count = lax.axis_size("region")
    region_idx = lax.axis_index("region")
    column_idx = lax.axis_index("rows")
    batches, obs_count = obs_order.shape
    slot_count = obs_count // group_size
    members = ensemble_state.shape[1]

    own_rows = lax.dynamic_slice_in_dim(obs_rows, column_idx * slot_count, slot_count, axis=1)
    pieces = ensemble_state[own_rows]
    pieces = pick_owner(pieces, batch_owner, "region")
    raw = lax.all_gather(pieces, "rows", axis=1, tiled=True)

    region_ids = jnp.arange(region_count, dtype=jnp.int32)
    reads = jnp.logical_or(
        region_ids[None, :] == batch_owner[:, None],
        jnp.any(readers[:, :, None] == region_ids[None, None, :], axis=1),
    )
    table = jnp.concatenate(
        [obs_values[:, :, None], obs_error[:, :, None], jnp.swapaxes(loc_taper, 1, 2)], axis=2
    )
    picks = (obs_order[:, :, None] == jnp.arange(obs_count, dtype=jnp.int32)).astype(jnp.float32)
    slot_table = jnp.einsum("bsj,bjc->bsc", picks, table, precision=lax.Precision.HIGHEST)
    slot_values = slot_table[:, :, 0]
    slot_errors = slot_table[:, :, 1]
    slot_taper = jnp.swapaxes(slot_table[:, :, 2 : 2 + region_count], 1, 2)

    pending = [raw[k] for k in range(batches)]
    scaled_list, incr_list = [], []
    for earlier in range(batches):
        scaled, obs_incr = adjust_rows(pending[earlier], slot_values[earlier], slot_errors[earlier])
        scaled_list.append(scaled)
        incr_list.append(obs_incr)
        later = list(range(earlier + 1, batches))
        if not later:
            break
        block_x = jnp.stack([pending[k] for k in later])
        weights = jnp.stack([slot_taper[earlier, batch_owner[k]] for k in later])
        applies = jnp.stack([reads[earlier, batch_owner[k]] for k in later])
        centre = jnp.mean(block_x, axis=2, keepdims=True)
        state_anom = (block_x - centre).astype(jnp.bfloat16)
        linked = jnp.einsum("kim,jm->kij", state_anom, scaled, preferred_element_type=jnp.float32)
        coupling = (linked * weights[:, None, :]).astype(jnp.bfloat16)
        moved = block_x + jnp.einsum("kij,jm->kim", coupling, obs_incr, preferred_element_type=jnp.float32)
        moved = jnp.where(applies[:, None, None], moved, block_x)
        for position, k in enumerate(later):
            pending[k] = moved[position]
    scaled_all = jnp.stack(scaled_list)
    incr_all = jnp.stack(incr_list)

    def main_step(batch_idx, current):
        weights = slot_taper[batch_idx, region_idx]
        return lax.cond(
            reads[batch_idx, region_idx],
            lambda rows_x: update_block(rows_x, scaled_all[batch_idx], incr_all[batch_idx], weights),
            lambda rows_x: rows_x,
            current,
        )

    current = lax.fori_loop(0, batches, main_step, ensemble_state)
    return current


def solution(mesh):
    placed = (P(("region", "rows"), None), P(), P(), P(), P(), P(), P(), P())
    return jax.shard_map(
        local, mesh=mesh, in_specs=placed, out_specs=P(("region", "rows"), None), check_vma=False
    )
```

```python
import jax
import jax.numpy as jnp
from jax import lax
from jax.experimental import pallas as pl
from jax.sharding import PartitionSpec as P


def adjust(prior_ens, values, errors):
    members = prior_ens.shape[1]
    prior_mean = jnp.mean(prior_ens, axis=1, keepdims=True)
    anomalies = prior_ens - prior_mean
    variance = jnp.sum(anomalies * anomalies, axis=1, keepdims=True) / (members - 1) + 1e-05
    errors = errors[:, None]
    values = values[:, None]
    post_var = variance * errors / (variance + errors)
    mean_shift = post_var * (prior_mean / variance + values / errors) - prior_mean
    shrink = jnp.sqrt(errors / (variance + errors))
    obs_incr = (mean_shift + (shrink - 1.0) * anomalies).astype(jnp.bfloat16)
    scaled = (anomalies / ((members - 1) * variance)).astype(jnp.bfloat16)
    return (scaled, obs_incr)


def adjust_kernel(prior_ref, values_ref, errors_ref, scaled_ref, incr_ref):
    scaled, obs_incr = adjust(prior_ref[...], values_ref[...][:, 0], errors_ref[...][:, 0])
    scaled_ref[...] = scaled
    incr_ref[...] = obs_incr


def adjust_rows(prior, values, errors, block=256):
    rows, members = prior.shape
    row_spec = pl.BlockSpec((block, members), lambda i: (i, 0))
    col_spec = pl.BlockSpec((block, 1), lambda i: (i, 0))
    out = jax.ShapeDtypeStruct((rows, members), jnp.bfloat16)
    return pl.pallas_call(
        adjust_kernel,
        grid=(rows // block,),
        in_specs=[row_spec, col_spec, col_spec],
        out_specs=[row_spec, row_spec],
        out_shape=[out, out],
    )(prior, values[:, None], errors[:, None])


def update_block(block_x, scaled, obs_incr, weights):
    centre = jnp.mean(block_x, axis=1, keepdims=True)
    state_anom = (block_x - centre).astype(jnp.bfloat16)
    linked = lax.dot_general(
        state_anom, scaled, (((1,), (1,)), ((), ())), preferred_element_type=jnp.float32
    )
    coupling = (linked * weights[None, :]).astype(jnp.bfloat16)
    return block_x + jnp.dot(coupling, obs_incr, preferred_element_type=jnp.float32)


def update_kernel(x_ref, scaled_ref, incr_ref, weights_ref, out_ref):
    current = x_ref[...]
    for batch_idx in range(scaled_ref.shape[0]):
        centre = jnp.mean(current, axis=1, keepdims=True)
        state_anom = (current - centre).astype(jnp.bfloat16)
        linked = lax.dot_general(
            state_anom, scaled_ref[batch_idx], (((1,), (1,)), ((), ())),
            preferred_element_type=jnp.float32,
        )
        coupling = (linked * weights_ref[0, batch_idx]).astype(jnp.bfloat16)
        current = current + jnp.dot(coupling, incr_ref[batch_idx], preferred_element_type=jnp.float32)
    out_ref[...] = current


def update_rows(block_x, scaled, obs_incr, weights, group_rows, block=256):
    rows, members = block_x.shape
    row_spec = pl.BlockSpec((block, members), lambda i: (i, 0))
    full_spec = pl.BlockSpec(scaled.shape, lambda i: (0, 0, 0))
    per_group = group_rows // block
    weight_spec = pl.BlockSpec((1,) + weights.shape[1:], lambda i: (i // per_group, 0, 0, 0))
    return pl.pallas_call(
        update_kernel,
        grid=(rows // block,),
        in_specs=[row_spec, full_spec, full_spec, weight_spec],
        out_specs=row_spec,
        out_shape=jax.ShapeDtypeStruct(block_x.shape, block_x.dtype),
    )(block_x, scaled, obs_incr, weights)


def pick_owner(pieces, owners, axis):
    size = lax.axis_size(axis)
    me = lax.axis_index(axis)
    held = pieces
    step = 1
    while step < size:
        partner = lax.ppermute(held, axis, [(i, i ^ step) for i in range(size)])
        keep = ((me // step) % 2) == ((owners // step) % 2)
        held = jnp.where(keep[:, None, None], held, partner)
        step *= 2
    return held


def local(
    ensemble_state, obs_values, obs_error, batch_owner, readers, obs_order, obs_rows, loc_taper
):
    group_size = lax.axis_size("rows")
    region_count = lax.axis_size("region")
    region_idx = lax.axis_index("region")
    column_idx = lax.axis_index("rows")
    batches, obs_count = obs_order.shape
    slot_count = obs_count // group_size
    members = ensemble_state.shape[1]

    own_rows = lax.dynamic_slice_in_dim(obs_rows, column_idx * slot_count, slot_count, axis=1)
    pieces = ensemble_state[own_rows]
    pieces = pick_owner(pieces, batch_owner, "region")
    raw = lax.all_gather(pieces, "rows", axis=1, tiled=True)

    region_ids = jnp.arange(region_count, dtype=jnp.int32)
    reads = jnp.logical_or(
        region_ids[None, :] == batch_owner[:, None],
        jnp.any(readers[:, :, None] == region_ids[None, None, :], axis=1),
    )
    table = jnp.concatenate(
        [obs_values[:, :, None], obs_error[:, :, None], jnp.swapaxes(loc_taper, 1, 2)], axis=2
    )
    picks = (obs_order[:, :, None] == jnp.arange(obs_count, dtype=jnp.int32)).astype(jnp.float32)
    slot_table = jnp.einsum("bsj,bjc->bsc", picks, table, precision=lax.Precision.HIGHEST)
    slot_values = slot_table[:, :, 0]
    slot_errors = slot_table[:, :, 1]
    slot_taper = jnp.swapaxes(slot_table[:, :, 2 : 2 + region_count], 1, 2)

    pending = [raw[k] for k in range(batches)]
    scaled_list, incr_list = [], []
    for earlier in range(batches):
        scaled, obs_incr = adjust_rows(pending[earlier], slot_values[earlier], slot_errors[earlier])
        scaled_list.append(scaled)
        incr_list.append(obs_incr)
        later = list(range(earlier + 1, batches))
        if not later:
            break
        block_x = jnp.concatenate([pending[k] for k in later])
        weights = jnp.stack(
            [
                jnp.where(reads[earlier, batch_owner[k]], slot_taper[earlier, batch_owner[k]], 0.0)
                for k in later
            ]
        )
        moved = update_rows(
            block_x, scaled[None], obs_incr[None], weights[:, None, None, :], obs_count
        ).reshape(len(later), obs_count, members)
        for position, k in enumerate(later):
            pending[k] = moved[position]
    scaled_all = jnp.stack(scaled_list)
    incr_all = jnp.stack(incr_list)

    main_weights = jnp.where(reads[:, region_idx, None], slot_taper[:, region_idx], 0.0)
    current = update_rows(
        ensemble_state, scaled_all, incr_all, main_weights[None, :, None, :], ensemble_state.shape[0]
    )
    return current


def solution(mesh):
    placed = (P(("region", "rows"), None), P(), P(), P(), P(), P(), P(), P())
    return jax.shard_map(
        local, mesh=mesh, in_specs=placed, out_specs=P(("region", "rows"), None), check_vma=False
    )
```

```python
import jax
import jax.numpy as jnp
from jax import lax
from jax.experimental import pallas as pl
from jax.sharding import PartitionSpec as P


def adjust(prior_ens, values, errors):
    members = prior_ens.shape[1]
    prior_mean = jnp.mean(prior_ens, axis=1, keepdims=True)
    anomalies = prior_ens - prior_mean
    variance = jnp.sum(anomalies * anomalies, axis=1, keepdims=True) / (members - 1) + 1e-05
    errors = errors[:, None]
    values = values[:, None]
    post_var = variance * errors / (variance + errors)
    mean_shift = post_var * (prior_mean / variance + values / errors) - prior_mean
    shrink = jnp.sqrt(errors / (variance + errors))
    obs_incr = (mean_shift + (shrink - 1.0) * anomalies).astype(jnp.bfloat16)
    scaled = (anomalies / ((members - 1) * variance)).astype(jnp.bfloat16)
    return (scaled, obs_incr)


def adjust_kernel(prior_ref, values_ref, errors_ref, scaled_ref, incr_ref):
    prior_ens = prior_ref[...]
    members = prior_ens.shape[1]
    values = values_ref[...]
    errors = errors_ref[...]
    prior_mean = jnp.mean(prior_ens, axis=1, keepdims=True)
    anomalies = prior_ens - prior_mean
    variance = jnp.sum(anomalies * anomalies, axis=1, keepdims=True) / (members - 1) + 1e-05
    post_var = variance * errors / (variance + errors)
    mean_shift = post_var * (prior_mean / variance + values / errors) - prior_mean
    shrink = jnp.sqrt(errors / (variance + errors))
    incr_ref[...] = (mean_shift + (shrink - 1.0) * anomalies).astype(jnp.bfloat16)
    inverse = 1.0 / ((members - 1) * variance)
    scaled_ref[...] = (anomalies * inverse).astype(jnp.bfloat16)


def adjust_rows(prior, values, errors, block=512):
    rows, members = prior.shape
    row_spec = pl.BlockSpec((block, members), lambda i: (i, 0))
    col_spec = pl.BlockSpec((block, 1), lambda i: (i, 0))
    out = jax.ShapeDtypeStruct((rows, members), jnp.bfloat16)
    return pl.pallas_call(
        adjust_kernel,
        grid=(rows // block,),
        in_specs=[row_spec, col_spec, col_spec],
        out_specs=[row_spec, row_spec],
        out_shape=[out, out],
    )(prior, values[:, None], errors[:, None])


def update_block(block_x, scaled, obs_incr, weights):
    centre = jnp.mean(block_x, axis=1, keepdims=True)
    state_anom = (block_x - centre).astype(jnp.bfloat16)
    linked = lax.dot_general(
        state_anom, scaled, (((1,), (1,)), ((), ())), preferred_element_type=jnp.float32
    )
    coupling = (linked * weights[None, :]).astype(jnp.bfloat16)
    return block_x + jnp.dot(coupling, obs_incr, preferred_element_type=jnp.float32)


def update_kernel(x_ref, scaled_ref, incr_ref, weights_ref, out_ref):
    current = x_ref[...]
    for batch_idx in range(scaled_ref.shape[0]):
        centre = jnp.mean(current, axis=1, keepdims=True)
        state_anom = (current - centre).astype(jnp.bfloat16)
        linked = jnp.dot(state_anom, scaled_ref[batch_idx], preferred_element_type=jnp.float32)
        coupling = (linked * weights_ref[0, batch_idx]).astype(jnp.bfloat16)
        current = current + jnp.dot(coupling, incr_ref[batch_idx], preferred_element_type=jnp.float32)
    out_ref[...] = current


def update_rows(block_x, scaled, obs_incr, weights, group_rows, block=256):
    rows, members = block_x.shape
    row_spec = pl.BlockSpec((block, members), lambda i: (i, 0))
    scaled_spec = pl.BlockSpec(scaled.shape, lambda i: (0, 0, 0))
    incr_spec = pl.BlockSpec(obs_incr.shape, lambda i: (0, 0, 0))
    per_group = group_rows // block
    weight_spec = pl.BlockSpec((1,) + weights.shape[1:], lambda i: (i // per_group, 0, 0, 0))
    return pl.pallas_call(
        update_kernel,
        grid=(rows // block,),
        in_specs=[row_spec, scaled_spec, incr_spec, weight_spec],
        out_specs=row_spec,
        out_shape=jax.ShapeDtypeStruct(block_x.shape, block_x.dtype),
    )(block_x, scaled, obs_incr, weights)


def pick_owner(pieces, owners, axis):
    size = lax.axis_size(axis)
    me = lax.axis_index(axis)
    held = pieces
    step = 1
    while step < size:
        partner = lax.ppermute(held, axis, [(i, i ^ step) for i in range(size)])
        keep = ((me // step) % 2) == ((owners // step) % 2)
        held = jnp.where(keep[:, None, None], held, partner)
        step *= 2
    return held


def local(
    ensemble_state, obs_values, obs_error, batch_owner, readers, obs_order, obs_rows, loc_taper
):
    group_size = lax.axis_size("rows")
    region_count = lax.axis_size("region")
    region_idx = lax.axis_index("region")
    column_idx = lax.axis_index("rows")
    batches, obs_count = obs_order.shape
    slot_count = obs_count // group_size
    members = ensemble_state.shape[1]

    own_rows = lax.dynamic_slice_in_dim(obs_rows, column_idx * slot_count, slot_count, axis=1)
    pieces = ensemble_state[own_rows]
    pieces = pick_owner(pieces, batch_owner, "region")
    raw = lax.all_gather(pieces, "rows", axis=1, tiled=True)

    region_ids = jnp.arange(region_count, dtype=jnp.int32)
    reads = jnp.logical_or(
        region_ids[None, :] == batch_owner[:, None],
        jnp.any(readers[:, :, None] == region_ids[None, None, :], axis=1),
    )
    table = jnp.concatenate(
        [obs_values[:, :, None], obs_error[:, :, None], jnp.swapaxes(loc_taper, 1, 2)], axis=2
    )
    picks = (obs_order[:, :, None] == jnp.arange(obs_count, dtype=jnp.int32)).astype(jnp.float32)
    slot_table = jnp.einsum("bsj,bjc->bsc", picks, table, precision=lax.Precision.HIGHEST)
    slot_values = slot_table[:, :, 0]
    slot_errors = slot_table[:, :, 1]
    slot_taper = jnp.swapaxes(slot_table[:, :, 2 : 2 + region_count], 1, 2)

    pending = [raw[k] for k in range(batches)]
    scaled_list, incr_list = [], []
    for earlier in range(batches):
        scaled, obs_incr = adjust_rows(pending[earlier], slot_values[earlier], slot_errors[earlier])
        scaled_list.append(scaled)
        incr_list.append(obs_incr)
        later = list(range(earlier + 1, batches))
        if not later:
            break
        block_x = jnp.concatenate([pending[k] for k in later])
        weights = jnp.stack(
            [
                jnp.where(reads[earlier, batch_owner[k]], slot_taper[earlier, batch_owner[k]], 0.0)
                for k in later
            ]
        )
        moved = update_rows(
            block_x, scaled.T[None], obs_incr[None], weights[:, None, None, :], obs_count
        ).reshape(len(later), obs_count, members)
        for position, k in enumerate(later):
            pending[k] = moved[position]
    scaled_all = jnp.swapaxes(jnp.stack(scaled_list), 1, 2)
    incr_all = jnp.stack(incr_list)

    main_weights = jnp.where(reads[:, region_idx, None], slot_taper[:, region_idx], 0.0)
    current = update_rows(
        ensemble_state, scaled_all, incr_all, main_weights[None, :, None, :], ensemble_state.shape[0]
    )
    return current


def solution(mesh):
    placed = (P(("region", "rows"), None), P(), P(), P(), P(), P(), P(), P())
    return jax.shard_map(
        local, mesh=mesh, in_specs=placed, out_specs=P(("region", "rows"), None), check_vma=False
    )
```

```python
import jax
import jax.numpy as jnp
from jax import lax
from jax.experimental import pallas as pl
from jax.experimental.pallas import tpu as pltpu
from jax.sharding import PartitionSpec as P


def adjust(prior_ens, values, errors):
    members = prior_ens.shape[1]
    prior_mean = jnp.mean(prior_ens, axis=1, keepdims=True)
    anomalies = prior_ens - prior_mean
    variance = jnp.sum(anomalies * anomalies, axis=1, keepdims=True) / (members - 1) + 1e-05
    errors = errors[:, None]
    values = values[:, None]
    post_var = variance * errors / (variance + errors)
    mean_shift = post_var * (prior_mean / variance + values / errors) - prior_mean
    shrink = jnp.sqrt(errors / (variance + errors))
    obs_incr = (mean_shift + (shrink - 1.0) * anomalies).astype(jnp.bfloat16)
    scaled = (anomalies / ((members - 1) * variance)).astype(jnp.bfloat16)
    return (scaled, obs_incr)


def adjust_kernel(prior_ref, values_ref, errors_ref, scaled_ref, incr_ref):
    prior_ens = prior_ref[...]
    members = prior_ens.shape[1]
    values = values_ref[...]
    errors = errors_ref[...]
    prior_mean = jnp.mean(prior_ens, axis=1, keepdims=True)
    anomalies = prior_ens - prior_mean
    variance = jnp.sum(anomalies * anomalies, axis=1, keepdims=True) / (members - 1) + 1e-05
    post_var = variance * errors / (variance + errors)
    mean_shift = post_var * (prior_mean / variance + values / errors) - prior_mean
    shrink = jnp.sqrt(errors / (variance + errors))
    incr_ref[...] = (mean_shift + (shrink - 1.0) * anomalies).astype(jnp.bfloat16)
    inverse = 1.0 / ((members - 1) * variance)
    scaled_ref[...] = (anomalies * inverse).astype(jnp.bfloat16)


def adjust_rows(prior, values, errors, block=512):
    rows, members = prior.shape
    row_spec = pl.BlockSpec((block, members), lambda i: (i, 0))
    col_spec = pl.BlockSpec((block, 1), lambda i: (i, 0))
    out = jax.ShapeDtypeStruct((rows, members), jnp.bfloat16)
    return pl.pallas_call(
        adjust_kernel,
        grid=(rows // block,),
        in_specs=[row_spec, col_spec, col_spec],
        out_specs=[row_spec, row_spec],
        out_shape=[out, out],
    )(prior, values[:, None], errors[:, None])


def update_block(block_x, scaled, obs_incr, weights):
    centre = jnp.mean(block_x, axis=1, keepdims=True)
    state_anom = (block_x - centre).astype(jnp.bfloat16)
    linked = lax.dot_general(
        state_anom, scaled, (((1,), (1,)), ((), ())), preferred_element_type=jnp.float32
    )
    coupling = (linked * weights[None, :]).astype(jnp.bfloat16)
    return block_x + jnp.dot(coupling, obs_incr, preferred_element_type=jnp.float32)


def update_kernel(flags_ref, x_ref, scaled_ref, incr_ref, weights_ref, out_ref):
    out_ref[...] = x_ref[...]
    for batch_idx in range(scaled_ref.shape[0]):

        @pl.when(flags_ref[batch_idx] != 0)
        def _(batch_idx=batch_idx):
            current = out_ref[...]
            centre = jnp.mean(current, axis=1, keepdims=True)
            state_anom = (current - centre).astype(jnp.bfloat16)
            linked = lax.dot_general(
                state_anom, scaled_ref[batch_idx], (((1,), (1,)), ((), ())),
                preferred_element_type=jnp.float32,
            )
            coupling = (linked * weights_ref[0, batch_idx]).astype(jnp.bfloat16)
            out_ref[...] = current + jnp.dot(
                coupling, incr_ref[batch_idx], preferred_element_type=jnp.float32
            )


def update_rows(block_x, scaled, obs_incr, weights, flags, group_rows, block=256):
    rows, members = block_x.shape
    row_spec = pl.BlockSpec((block, members), lambda i, f: (i, 0))
    full_spec = pl.BlockSpec(scaled.shape, lambda i, f: (0, 0, 0))
    per_group = group_rows // block
    weight_spec = pl.BlockSpec((1,) + weights.shape[1:], lambda i, f: (i // per_group, 0, 0, 0))
    return pl.pallas_call(
        update_kernel,
        grid_spec=pltpu.PrefetchScalarGridSpec(
            num_scalar_prefetch=1,
            grid=(rows // block,),
            in_specs=[row_spec, full_spec, full_spec, weight_spec],
            out_specs=row_spec,
        ),
        out_shape=jax.ShapeDtypeStruct(block_x.shape, block_x.dtype),
    )(flags.astype(jnp.int32), block_x, scaled, obs_incr, weights)


def pick_owner(pieces, owners, axis):
    size = lax.axis_size(axis)
    me = lax.axis_index(axis)
    held = pieces
    step = 1
    while step < size:
        partner = lax.ppermute(held, axis, [(i, i ^ step) for i in range(size)])
        keep = ((me // step) % 2) == ((owners // step) % 2)
        held = jnp.where(keep[:, None, None], held, partner)
        step *= 2
    return held


def local(
    ensemble_state, obs_values, obs_error, batch_owner, readers, obs_order, obs_rows, loc_taper
):
    group_size = lax.axis_size("rows")
    region_count = lax.axis_size("region")
    region_idx = lax.axis_index("region")
    column_idx = lax.axis_index("rows")
    batches, obs_count = obs_order.shape
    slot_count = obs_count // group_size
    members = ensemble_state.shape[1]

    own_rows = lax.dynamic_slice_in_dim(obs_rows, column_idx * slot_count, slot_count, axis=1)
    pieces = ensemble_state[own_rows]
    pieces = pick_owner(pieces, batch_owner, "region")
    raw = lax.all_gather(pieces, "rows", axis=1, tiled=True)

    region_ids = jnp.arange(region_count, dtype=jnp.int32)
    reads = jnp.logical_or(
        region_ids[None, :] == batch_owner[:, None],
        jnp.any(readers[:, :, None] == region_ids[None, None, :], axis=1),
    )
    table = jnp.concatenate(
        [obs_values[:, :, None], obs_error[:, :, None], jnp.swapaxes(loc_taper, 1, 2)], axis=2
    )
    picks = (obs_order[:, :, None] == jnp.arange(obs_count, dtype=jnp.int32)).astype(jnp.float32)
    slot_table = jnp.einsum("bsj,bjc->bsc", picks, table, precision=lax.Precision.HIGHEST)
    slot_values = slot_table[:, :, 0]
    slot_errors = slot_table[:, :, 1]
    slot_taper = jnp.swapaxes(slot_table[:, :, 2 : 2 + region_count], 1, 2)

    pending = [raw[k] for k in range(batches)]
    scaled_list, incr_list = [], []
    for earlier in range(batches):
        scaled, obs_incr = adjust_rows(pending[earlier], slot_values[earlier], slot_errors[earlier])
        scaled_list.append(scaled)
        incr_list.append(obs_incr)
        later = list(range(earlier + 1, batches))
        if not later:
            break
        for k in later:
            owner = batch_owner[k]
            pending[k] = lax.cond(
                reads[earlier, owner],
                lambda rows_x, s=scaled, o=obs_incr, w=slot_taper[earlier, owner]: update_rows(
                    rows_x, s[None], o[None], w[None, None, None, :], jnp.ones((1,), jnp.int32),
                    obs_count,
                ),
                lambda rows_x: rows_x,
                pending[k],
            )
    scaled_all = jnp.stack(scaled_list)
    incr_all = jnp.stack(incr_list)

    main_weights = jnp.where(reads[:, region_idx, None], slot_taper[:, region_idx], 0.0)
    current = update_rows(
        ensemble_state, scaled_all, incr_all, main_weights[None, :, None, :],
        reads[:, region_idx], ensemble_state.shape[0],
    )
    return current


def solution(mesh):
    placed = (P(("region", "rows"), None), P(), P(), P(), P(), P(), P(), P())
    return jax.shard_map(
        local, mesh=mesh, in_specs=placed, out_specs=P(("region", "rows"), None), check_vma=False
    )
```

```python
import jax
import jax.numpy as jnp
from jax import lax
from jax.experimental import pallas as pl
from jax.experimental.pallas import tpu as pltpu
from jax.sharding import PartitionSpec as P


def adjust(prior_ens, values, errors):
    members = prior_ens.shape[1]
    prior_mean = jnp.mean(prior_ens, axis=1, keepdims=True)
    anomalies = prior_ens - prior_mean
    variance = jnp.sum(anomalies * anomalies, axis=1, keepdims=True) / (members - 1) + 1e-05
    errors = errors[:, None]
    values = values[:, None]
    post_var = variance * errors / (variance + errors)
    mean_shift = post_var * (prior_mean / variance + values / errors) - prior_mean
    shrink = jnp.sqrt(errors / (variance + errors))
    obs_incr = (mean_shift + (shrink - 1.0) * anomalies).astype(jnp.bfloat16)
    scaled = (anomalies / ((members - 1) * variance)).astype(jnp.bfloat16)
    return (scaled, obs_incr)


def adjust_kernel(prior_ref, values_ref, errors_ref, scaled_ref, incr_ref):
    prior_ens = prior_ref[...]
    members = prior_ens.shape[1]
    values = values_ref[...]
    errors = errors_ref[...]
    prior_mean = jnp.mean(prior_ens, axis=1, keepdims=True)
    anomalies = prior_ens - prior_mean
    variance = jnp.sum(anomalies * anomalies, axis=1, keepdims=True) / (members - 1) + 1e-05
    post_var = variance * errors / (variance + errors)
    mean_shift = post_var * (prior_mean / variance + values / errors) - prior_mean
    shrink = jnp.sqrt(errors / (variance + errors))
    incr_ref[...] = (mean_shift + (shrink - 1.0) * anomalies).astype(jnp.bfloat16)
    inverse = 1.0 / ((members - 1) * variance)
    scaled_ref[...] = (anomalies * inverse).astype(jnp.bfloat16)


def adjust_rows(prior, values, errors, block=512):
    rows, members = prior.shape
    row_spec = pl.BlockSpec((block, members), lambda i: (i, 0))
    col_spec = pl.BlockSpec((block, 1), lambda i: (i, 0))
    out = jax.ShapeDtypeStruct((rows, members), jnp.bfloat16)
    return pl.pallas_call(
        adjust_kernel,
        grid=(rows // block,),
        in_specs=[row_spec, col_spec, col_spec],
        out_specs=[row_spec, row_spec],
        out_shape=[out, out],
    )(prior, values[:, None], errors[:, None])


def update_block(block_x, scaled, obs_incr, weights):
    centre = jnp.mean(block_x, axis=1, keepdims=True)
    state_anom = (block_x - centre).astype(jnp.bfloat16)
    linked = lax.dot_general(
        state_anom, scaled, (((1,), (1,)), ((), ())), preferred_element_type=jnp.float32
    )
    coupling = (linked * weights[None, :]).astype(jnp.bfloat16)
    return block_x + jnp.dot(coupling, obs_incr, preferred_element_type=jnp.float32)


def update_kernel(flags_ref, x_ref, scaled_ref, incr_ref, weights_ref, out_ref):
    out_ref[...] = x_ref[...]
    for batch_idx in range(scaled_ref.shape[0]):

        @pl.when(flags_ref[batch_idx] != 0)
        def _(batch_idx=batch_idx):
            current = out_ref[...]
            centre = jnp.mean(current, axis=1, keepdims=True)
            state_anom = (current - centre).astype(jnp.bfloat16)
            linked = lax.dot_general(
                state_anom, scaled_ref[batch_idx], (((1,), (1,)), ((), ())),
                preferred_element_type=jnp.float32,
            )
            coupling = (linked * weights_ref[0, batch_idx]).astype(jnp.bfloat16)
            out_ref[...] = current + jnp.dot(
                coupling, incr_ref[batch_idx], preferred_element_type=jnp.float32
            )


def update_rows(block_x, scaled, obs_incr, weights, flags, group_rows, block=256):
    rows, members = block_x.shape
    row_spec = pl.BlockSpec((block, members), lambda i, f: (i, 0))
    full_spec = pl.BlockSpec(scaled.shape, lambda i, f: (0, 0, 0))
    per_group = group_rows // block
    weight_spec = pl.BlockSpec((1,) + weights.shape[1:], lambda i, f: (i // per_group, 0, 0, 0))
    return pl.pallas_call(
        update_kernel,
        grid_spec=pltpu.PrefetchScalarGridSpec(
            num_scalar_prefetch=1,
            grid=(rows // block,),
            in_specs=[row_spec, full_spec, full_spec, weight_spec],
            out_specs=row_spec,
        ),
        out_shape=jax.ShapeDtypeStruct(block_x.shape, block_x.dtype),
    )(flags.astype(jnp.int32), block_x, scaled, obs_incr, weights)


def pick_owner(pieces, owners, axis):
    size = lax.axis_size(axis)
    me = lax.axis_index(axis)
    held = pieces
    step = 1
    while step < size:
        partner = lax.ppermute(held, axis, [(i, i ^ step) for i in range(size)])
        keep = ((me // step) % 2) == ((owners // step) % 2)
        held = jnp.where(keep[:, None, None], held, partner)
        step *= 2
    return held


def gather_rows(pieces, axis):
    size = lax.axis_size(axis)
    me = lax.axis_index(axis)
    width = pieces.shape[1]
    held = jnp.zeros(pieces.shape[:1] + (size * width,) + pieces.shape[2:], pieces.dtype)
    held = lax.dynamic_update_slice_in_dim(held, pieces, me * width, axis=1)
    step = 1
    while step < size:
        base = (me // step) * step * width
        mine = lax.dynamic_slice_in_dim(held, base, step * width, axis=1)
        theirs = lax.ppermute(mine, axis, [(i, i ^ step) for i in range(size)])
        other = ((me // step) ^ 1) * step * width
        held = lax.dynamic_update_slice_in_dim(held, theirs, other, axis=1)
        step *= 2
    return held


def local(
    ensemble_state, obs_values, obs_error, batch_owner, readers, obs_order, obs_rows, loc_taper
):
    group_size = lax.axis_size("rows")
    region_count = lax.axis_size("region")
    region_idx = lax.axis_index("region")
    column_idx = lax.axis_index("rows")
    batches, obs_count = obs_order.shape
    slot_count = obs_count // group_size
    members = ensemble_state.shape[1]

    own_rows = lax.dynamic_slice_in_dim(obs_rows, column_idx * slot_count, slot_count, axis=1)
    pieces = ensemble_state[own_rows]
    pieces = pick_owner(pieces, batch_owner, "region")
    raw = gather_rows(pieces, "rows")

    region_ids = jnp.arange(region_count, dtype=jnp.int32)
    reads = jnp.logical_or(
        region_ids[None, :] == batch_owner[:, None],
        jnp.any(readers[:, :, None] == region_ids[None, None, :], axis=1),
    )
    table = jnp.concatenate(
        [obs_values[:, :, None], obs_error[:, :, None], jnp.swapaxes(loc_taper, 1, 2)], axis=2
    )
    picks = (obs_order[:, :, None] == jnp.arange(obs_count, dtype=jnp.int32)).astype(jnp.float32)
    slot_table = jnp.einsum("bsj,bjc->bsc", picks, table, precision=lax.Precision.HIGHEST)
    slot_values = slot_table[:, :, 0]
    slot_errors = slot_table[:, :, 1]
    slot_taper = jnp.swapaxes(slot_table[:, :, 2 : 2 + region_count], 1, 2)

    pending = [raw[k] for k in range(batches)]
    scaled_list, incr_list = [], []
    for earlier in range(batches):
        scaled, obs_incr = adjust_rows(pending[earlier], slot_values[earlier], slot_errors[earlier])
        scaled_list.append(scaled)
        incr_list.append(obs_incr)
        later = list(range(earlier + 1, batches))
        if not later:
            break
        for k in later:
            owner = batch_owner[k]
            pending[k] = lax.cond(
                reads[earlier, owner],
                lambda rows_x, s=scaled, o=obs_incr, w=slot_taper[earlier, owner]: update_rows(
                    rows_x, s[None], o[None], w[None, None, None, :], jnp.ones((1,), jnp.int32),
                    obs_count,
                ),
                lambda rows_x: rows_x,
                pending[k],
            )
    scaled_all = jnp.stack(scaled_list)
    incr_all = jnp.stack(incr_list)

    main_weights = jnp.where(reads[:, region_idx, None], slot_taper[:, region_idx], 0.0)
    current = update_rows(
        ensemble_state, scaled_all, incr_all, main_weights[None, :, None, :],
        reads[:, region_idx], ensemble_state.shape[0],
    )
    return current


def solution(mesh):
    placed = (P(("region", "rows"), None), P(), P(), P(), P(), P(), P(), P())
    return jax.shard_map(
        local, mesh=mesh, in_specs=placed, out_specs=P(("region", "rows"), None), check_vma=False
    )
```

```python
import functools

import jax
import jax.numpy as jnp
from jax import lax
from jax.experimental import pallas as pl
from jax.experimental.pallas import tpu as pltpu
from jax.sharding import PartitionSpec as P


def adjust(prior_ens, values, errors):
    members = prior_ens.shape[1]
    prior_mean = jnp.mean(prior_ens, axis=1, keepdims=True)
    anomalies = prior_ens - prior_mean
    variance = jnp.sum(anomalies * anomalies, axis=1, keepdims=True) / (members - 1) + 1e-05
    errors = errors[:, None]
    values = values[:, None]
    post_var = variance * errors / (variance + errors)
    mean_shift = post_var * (prior_mean / variance + values / errors) - prior_mean
    shrink = jnp.sqrt(errors / (variance + errors))
    obs_incr = (mean_shift + (shrink - 1.0) * anomalies).astype(jnp.bfloat16)
    scaled = (anomalies / ((members - 1) * variance)).astype(jnp.bfloat16)
    return (scaled, obs_incr)


def adjust_kernel(prior_ref, values_ref, errors_ref, scaled_ref, incr_ref):
    prior_ens = prior_ref[...]
    members = prior_ens.shape[1]
    values = values_ref[...]
    errors = errors_ref[...]
    prior_mean = jnp.mean(prior_ens, axis=1, keepdims=True)
    anomalies = prior_ens - prior_mean
    variance = jnp.sum(anomalies * anomalies, axis=1, keepdims=True) / (members - 1) + 1e-05
    post_var = variance * errors / (variance + errors)
    mean_shift = post_var * (prior_mean / variance + values / errors) - prior_mean
    shrink = jnp.sqrt(errors / (variance + errors))
    incr_ref[...] = (mean_shift + (shrink - 1.0) * anomalies).astype(jnp.bfloat16)
    inverse = 1.0 / ((members - 1) * variance)
    scaled_ref[...] = (anomalies * inverse).astype(jnp.bfloat16)


def adjust_rows(source, index, values, errors, block=512):
    _, rows, members = source.shape
    in_spec = pl.BlockSpec((None, block, members), lambda i: (index, i, 0))
    row_spec = pl.BlockSpec((block, members), lambda i: (i, 0))
    col_spec = pl.BlockSpec((block, 1), lambda i: (i, 0))
    out = jax.ShapeDtypeStruct((rows, members), jnp.bfloat16)
    return pl.pallas_call(
        adjust_kernel,
        grid=(rows // block,),
        in_specs=[in_spec, col_spec, col_spec],
        out_specs=[row_spec, row_spec],
        out_shape=[out, out],
    )(source, values[:, None], errors[:, None])


def update_kernel(batches, flags_ref, x_ref, *refs):
    scaled_refs = refs[:batches]
    incr_refs = refs[batches : 2 * batches]
    weights_ref = refs[2 * batches]
    out_ref = refs[2 * batches + 1]
    out_ref[...] = x_ref[...]
    for batch_idx in range(batches):

        @pl.when(flags_ref[batch_idx] != 0)
        def _(batch_idx=batch_idx):
            current = out_ref[...]
            centre = jnp.mean(current, axis=1, keepdims=True)
            state_anom = (current - centre).astype(jnp.bfloat16)
            linked = lax.dot_general(
                state_anom, scaled_refs[batch_idx][...], (((1,), (1,)), ((), ())),
                preferred_element_type=jnp.float32,
            )
            coupling = (linked * weights_ref[0, batch_idx]).astype(jnp.bfloat16)
            out_ref[...] = current + jnp.dot(
                coupling, incr_refs[batch_idx][...], preferred_element_type=jnp.float32
            )


def update_rows(source, index, scaled, obs_incr, weights, flags, group_rows, block=256):
    _, rows, members = source.shape
    batches = len(scaled)
    in_spec = pl.BlockSpec((None, block, members), lambda i, f: (index, i, 0))
    row_spec = pl.BlockSpec((block, members), lambda i, f: (i, 0))
    full_spec = pl.BlockSpec(scaled[0].shape, lambda i, f: (0, 0))
    per_group = group_rows // block
    weight_spec = pl.BlockSpec((1,) + weights.shape[1:], lambda i, f: (i // per_group, 0, 0, 0))
    return pl.pallas_call(
        functools.partial(update_kernel, batches),
        grid_spec=pltpu.PrefetchScalarGridSpec(
            num_scalar_prefetch=1,
            grid=(rows // block,),
            in_specs=[in_spec] + [full_spec] * (2 * batches) + [weight_spec],
            out_specs=row_spec,
        ),
        out_shape=jax.ShapeDtypeStruct((rows, members), source.dtype),
    )(flags.astype(jnp.int32), source, *scaled, *obs_incr, weights)


def pick_owner(pieces, owners, axis):
    size = lax.axis_size(axis)
    me = lax.axis_index(axis)
    held = pieces
    step = 1
    while step < size:
        partner = lax.ppermute(held, axis, [(i, i ^ step) for i in range(size)])
        keep = ((me // step) % 2) == ((owners // step) % 2)
        held = jnp.where(keep[:, None, None], held, partner)
        step *= 2
    return held


def local(
    ensemble_state, obs_values, obs_error, batch_owner, readers, obs_order, obs_rows, loc_taper
):
    group_size = lax.axis_size("rows")
    region_count = lax.axis_size("region")
    region_idx = lax.axis_index("region")
    column_idx = lax.axis_index("rows")
    batches, obs_count = obs_order.shape
    slot_count = obs_count // group_size
    members = ensemble_state.shape[1]

    own_rows = lax.dynamic_slice_in_dim(obs_rows, column_idx * slot_count, slot_count, axis=1)
    pieces = ensemble_state[own_rows]
    pieces = pick_owner(pieces, batch_owner, "region")
    raw = lax.all_gather(pieces, "rows", axis=1, tiled=True)

    region_ids = jnp.arange(region_count, dtype=jnp.int32)
    reads = jnp.logical_or(
        region_ids[None, :] == batch_owner[:, None],
        jnp.any(readers[:, :, None] == region_ids[None, None, :], axis=1),
    )
    table = jnp.concatenate(
        [obs_values[:, :, None], obs_error[:, :, None], jnp.swapaxes(loc_taper, 1, 2)], axis=2
    )
    picks = (obs_order[:, :, None] == jnp.arange(obs_count, dtype=jnp.int32)).astype(jnp.float32)
    slot_table = jnp.einsum("bsj,bjc->bsc", picks, table, precision=lax.Precision.HIGHEST)
    slot_values = slot_table[:, :, 0]
    slot_errors = slot_table[:, :, 1]
    slot_taper = jnp.swapaxes(slot_table[:, :, 2 : 2 + region_count], 1, 2)

    pending = [(raw, k) for k in range(batches)]
    scaled_list, incr_list = [], []
    for earlier in range(batches):
        source, index = pending[earlier]
        scaled, obs_incr = adjust_rows(source, index, slot_values[earlier], slot_errors[earlier])
        scaled_list.append(scaled)
        incr_list.append(obs_incr)
        for k in range(earlier + 1, batches):
            owner = batch_owner[k]
            source, index = pending[k]
            moved = lax.cond(
                reads[earlier, owner],
                lambda rows_x, s=scaled, o=obs_incr, w=slot_taper[earlier, owner], i=index: update_rows(
                    rows_x, i, [s], [o], w[None, None, None, :], jnp.ones((1,), jnp.int32),
                    obs_count, block=512,
                ),
                lambda rows_x, i=index: rows_x[i],
                source,
            )
            pending[k] = (moved[None], 0)

    main_weights = jnp.where(reads[:, region_idx, None], slot_taper[:, region_idx], 0.0)
    current = update_rows(
        ensemble_state[None], 0, scaled_list, incr_list, main_weights[None, :, None, :],
        reads[:, region_idx], ensemble_state.shape[0],
    )
    return current


def solution(mesh):
    placed = (P(("region", "rows"), None), P(), P(), P(), P(), P(), P(), P())
    return jax.shard_map(
        local, mesh=mesh, in_specs=placed, out_specs=P(("region", "rows"), None), check_vma=False
    )
```

```python
import functools

import jax
import jax.numpy as jnp
from jax import lax
from jax.experimental import pallas as pl
from jax.experimental.pallas import tpu as pltpu
from jax.sharding import PartitionSpec as P


def adjust(prior_ens, values, errors):
    members = prior_ens.shape[1]
    prior_mean = jnp.mean(prior_ens, axis=1, keepdims=True)
    anomalies = prior_ens - prior_mean
    variance = jnp.sum(anomalies * anomalies, axis=1, keepdims=True) / (members - 1) + 1e-05
    errors = errors[:, None]
    values = values[:, None]
    post_var = variance * errors / (variance + errors)
    mean_shift = post_var * (prior_mean / variance + values / errors) - prior_mean
    shrink = jnp.sqrt(errors / (variance + errors))
    obs_incr = (mean_shift + (shrink - 1.0) * anomalies).astype(jnp.bfloat16)
    scaled = (anomalies / ((members - 1) * variance)).astype(jnp.bfloat16)
    return (scaled, obs_incr)


def adjust_kernel(prior_ref, values_ref, errors_ref, scaled_ref, incr_ref):
    prior_ens = prior_ref[...]
    members = prior_ens.shape[1]
    values = values_ref[...]
    errors = errors_ref[...]
    prior_mean = jnp.mean(prior_ens, axis=1, keepdims=True)
    anomalies = prior_ens - prior_mean
    variance = jnp.sum(anomalies * anomalies, axis=1, keepdims=True) / (members - 1) + 1e-05
    post_var = variance * errors / (variance + errors)
    mean_shift = post_var * (prior_mean / variance + values / errors) - prior_mean
    shrink = jnp.sqrt(errors / (variance + errors))
    incr_ref[...] = (mean_shift + (shrink - 1.0) * anomalies).astype(jnp.bfloat16)
    inverse = 1.0 / ((members - 1) * variance)
    scaled_ref[...] = (anomalies * inverse).astype(jnp.bfloat16)


def adjust_rows(source, index, values, errors, block=512):
    _, rows, members = source.shape
    in_spec = pl.BlockSpec((None, block, members), lambda i: (index, i, 0))
    row_spec = pl.BlockSpec((block, members), lambda i: (i, 0))
    col_spec = pl.BlockSpec((block, 1), lambda i: (i, 0))
    out = jax.ShapeDtypeStruct((rows, members), jnp.bfloat16)
    return pl.pallas_call(
        adjust_kernel,
        grid=(rows // block,),
        in_specs=[in_spec, col_spec, col_spec],
        out_specs=[row_spec, row_spec],
        out_shape=[out, out],
    )(source, values[:, None], errors[:, None])


def update_kernel(batches, flags_ref, x_ref, *refs):
    scaled_refs = refs[:batches]
    incr_refs = refs[batches : 2 * batches]
    weights_ref = refs[2 * batches]
    out_ref = refs[2 * batches + 1]
    out_ref[...] = x_ref[...]
    for batch_idx in range(batches):

        @pl.when(flags_ref[batch_idx] != 0)
        def _(batch_idx=batch_idx):
            current = out_ref[...]
            centre = jnp.mean(current, axis=1, keepdims=True)
            state_anom = (current - centre).astype(jnp.bfloat16)
            linked = lax.dot_general(
                state_anom, scaled_refs[batch_idx][...], (((1,), (1,)), ((), ())),
                preferred_element_type=jnp.float32,
            )
            coupling = (linked * weights_ref[0, batch_idx]).astype(jnp.bfloat16)
            out_ref[...] = current + jnp.dot(
                coupling, incr_refs[batch_idx][...], preferred_element_type=jnp.float32
            )


def update_rows(source, index, scaled, obs_incr, weights, flags, group_rows, block=256):
    _, rows, members = source.shape
    batches = len(scaled)
    in_spec = pl.BlockSpec((None, block, members), lambda i, f: (index, i, 0))
    row_spec = pl.BlockSpec((block, members), lambda i, f: (i, 0))
    full_spec = pl.BlockSpec(scaled[0].shape, lambda i, f: (0, 0))
    per_group = group_rows // block
    weight_spec = pl.BlockSpec((1,) + weights.shape[1:], lambda i, f: (i // per_group, 0, 0, 0))
    return pl.pallas_call(
        functools.partial(update_kernel, batches),
        grid_spec=pltpu.PrefetchScalarGridSpec(
            num_scalar_prefetch=1,
            grid=(rows // block,),
            in_specs=[in_spec] + [full_spec] * (2 * batches) + [weight_spec],
            out_specs=row_spec,
        ),
        out_shape=jax.ShapeDtypeStruct((rows, members), source.dtype),
    )(flags.astype(jnp.int32), source, *scaled, *obs_incr, weights)


def pick_owner(pieces, owners, axis):
    size = lax.axis_size(axis)
    me = lax.axis_index(axis)
    received = [pieces] + [
        lax.ppermute(pieces, axis, [(i, (i + shift) % size) for i in range(size)])
        for shift in range(1, size)
    ]
    shifts = (me - owners) % size
    held = pieces
    for shift in range(1, size):
        held = jnp.where((shifts == shift)[:, None, None], received[shift], held)
    return held


def local(
    ensemble_state, obs_values, obs_error, batch_owner, readers, obs_order, obs_rows, loc_taper
):
    group_size = lax.axis_size("rows")
    region_count = lax.axis_size("region")
    region_idx = lax.axis_index("region")
    column_idx = lax.axis_index("rows")
    batches, obs_count = obs_order.shape
    slot_count = obs_count // group_size
    members = ensemble_state.shape[1]

    own_rows = lax.dynamic_slice_in_dim(obs_rows, column_idx * slot_count, slot_count, axis=1)
    pieces = ensemble_state[own_rows]
    pieces = pick_owner(pieces, batch_owner, "region")
    raw = lax.all_gather(pieces, "rows", axis=1, tiled=True)

    region_ids = jnp.arange(region_count, dtype=jnp.int32)
    reads = jnp.logical_or(
        region_ids[None, :] == batch_owner[:, None],
        jnp.any(readers[:, :, None] == region_ids[None, None, :], axis=1),
    )
    table = jnp.concatenate(
        [obs_values[:, :, None], obs_error[:, :, None], jnp.swapaxes(loc_taper, 1, 2)], axis=2
    )
    picks = (obs_order[:, :, None] == jnp.arange(obs_count, dtype=jnp.int32)).astype(jnp.float32)
    slot_table = jnp.einsum("bsj,bjc->bsc", picks, table, precision=lax.Precision.HIGHEST)
    slot_values = slot_table[:, :, 0]
    slot_errors = slot_table[:, :, 1]
    slot_taper = jnp.swapaxes(slot_table[:, :, 2 : 2 + region_count], 1, 2)

    pending = [(raw, k) for k in range(batches)]
    scaled_list, incr_list = [], []
    for earlier in range(batches):
        source, index = pending[earlier]
        scaled, obs_incr = adjust_rows(source, index, slot_values[earlier], slot_errors[earlier])
        scaled_list.append(scaled)
        incr_list.append(obs_incr)
        for k in range(earlier + 1, batches):
            owner = batch_owner[k]
            source, index = pending[k]
            moved = lax.cond(
                reads[earlier, owner],
                lambda rows_x, s=scaled, o=obs_incr, w=slot_taper[earlier, owner], i=index: update_rows(
                    rows_x, i, [s], [o], w[None, None, None, :], jnp.ones((1,), jnp.int32),
                    obs_count, block=512,
                ),
                lambda rows_x, i=index: rows_x[i],
                source,
            )
            pending[k] = (moved[None], 0)

    main_weights = jnp.where(reads[:, region_idx, None], slot_taper[:, region_idx], 0.0)
    current = update_rows(
        ensemble_state[None], 0, scaled_list, incr_list, main_weights[None, :, None, :],
        reads[:, region_idx], ensemble_state.shape[0],
    )
    return current


def solution(mesh):
    placed = (P(("region", "rows"), None), P(), P(), P(), P(), P(), P(), P())
    return jax.shard_map(
        local, mesh=mesh, in_specs=placed, out_specs=P(("region", "rows"), None), check_vma=False
    )
```

```python
import functools

import jax
import jax.numpy as jnp
from jax import lax
from jax.experimental import pallas as pl
from jax.experimental.pallas import tpu as pltpu
from jax.sharding import PartitionSpec as P


def adjust(prior_ens, values, errors):
    members = prior_ens.shape[1]
    prior_mean = jnp.mean(prior_ens, axis=1, keepdims=True)
    anomalies = prior_ens - prior_mean
    variance = jnp.sum(anomalies * anomalies, axis=1, keepdims=True) / (members - 1) + 1e-05
    errors = errors[:, None]
    values = values[:, None]
    post_var = variance * errors / (variance + errors)
    mean_shift = post_var * (prior_mean / variance + values / errors) - prior_mean
    shrink = jnp.sqrt(errors / (variance + errors))
    obs_incr = (mean_shift + (shrink - 1.0) * anomalies).astype(jnp.bfloat16)
    scaled = (anomalies / ((members - 1) * variance)).astype(jnp.bfloat16)
    return (scaled, obs_incr)


def adjust_kernel(prior_ref, values_ref, errors_ref, scaled_ref, incr_ref):
    prior_ens = prior_ref[...]
    members = prior_ens.shape[1]
    values = values_ref[...]
    errors = errors_ref[...]
    prior_mean = jnp.mean(prior_ens, axis=1, keepdims=True)
    anomalies = prior_ens - prior_mean
    variance = jnp.sum(anomalies * anomalies, axis=1, keepdims=True) / (members - 1) + 1e-05
    post_var = variance * errors / (variance + errors)
    mean_shift = post_var * (prior_mean / variance + values / errors) - prior_mean
    shrink = jnp.sqrt(errors / (variance + errors))
    incr_ref[...] = (mean_shift + (shrink - 1.0) * anomalies).astype(jnp.bfloat16)
    inverse = 1.0 / ((members - 1) * variance)
    scaled_ref[...] = (anomalies * inverse).astype(jnp.bfloat16)


def adjust_rows(source, index, values, errors, block=1024):
    _, rows, members = source.shape
    in_spec = pl.BlockSpec((None, block, members), lambda i: (index, i, 0))
    row_spec = pl.BlockSpec((block, members), lambda i: (i, 0))
    col_spec = pl.BlockSpec((block, 1), lambda i: (i, 0))
    out = jax.ShapeDtypeStruct((rows, members), jnp.bfloat16)
    return pl.pallas_call(
        adjust_kernel,
        grid=(rows // block,),
        in_specs=[in_spec, col_spec, col_spec],
        out_specs=[row_spec, row_spec],
        out_shape=[out, out],
    )(source, values[:, None], errors[:, None])


def update_kernel(batches, flags_ref, x_ref, *refs):
    scaled_refs = refs[:batches]
    incr_refs = refs[batches : 2 * batches]
    weights_ref = refs[2 * batches]
    out_ref = refs[2 * batches + 1]
    out_ref[...] = x_ref[...]
    for batch_idx in range(batches):

        @pl.when(flags_ref[batch_idx] != 0)
        def _(batch_idx=batch_idx):
            current = out_ref[...]
            centre = jnp.mean(current, axis=1, keepdims=True)
            state_anom = (current - centre).astype(jnp.bfloat16)
            linked = lax.dot_general(
                state_anom, scaled_refs[batch_idx][...], (((1,), (1,)), ((), ())),
                preferred_element_type=jnp.float32,
            )
            coupling = (linked * weights_ref[0, batch_idx]).astype(jnp.bfloat16)
            out_ref[...] = current + jnp.dot(
                coupling, incr_refs[batch_idx][...], preferred_element_type=jnp.float32
            )


def update_rows(source, index, scaled, obs_incr, weights, flags, group_rows, block=256):
    _, rows, members = source.shape
    batches = len(scaled)
    in_spec = pl.BlockSpec((None, block, members), lambda i, f: (index, i, 0))
    row_spec = pl.BlockSpec((block, members), lambda i, f: (i, 0))
    full_spec = pl.BlockSpec(scaled[0].shape, lambda i, f: (0, 0))
    per_group = group_rows // block
    weight_spec = pl.BlockSpec((1,) + weights.shape[1:], lambda i, f: (i // per_group, 0, 0, 0))
    return pl.pallas_call(
        functools.partial(update_kernel, batches),
        grid_spec=pltpu.PrefetchScalarGridSpec(
            num_scalar_prefetch=1,
            grid=(rows // block,),
            in_specs=[in_spec] + [full_spec] * (2 * batches) + [weight_spec],
            out_specs=row_spec,
        ),
        out_shape=jax.ShapeDtypeStruct((rows, members), source.dtype),
    )(flags.astype(jnp.int32), source, *scaled, *obs_incr, weights)


def pick_owner(pieces, owners, axis):
    size = lax.axis_size(axis)
    me = lax.axis_index(axis)
    held = pieces
    step = 1
    while step < size:
        partner = lax.ppermute(held, axis, [(i, i ^ step) for i in range(size)])
        keep = ((me // step) % 2) == ((owners // step) % 2)
        held = jnp.where(keep[:, None, None], held, partner)
        step *= 2
    return held


def local(
    ensemble_state, obs_values, obs_error, batch_owner, readers, obs_order, obs_rows, loc_taper
):
    group_size = lax.axis_size("rows")
    region_count = lax.axis_size("region")
    region_idx = lax.axis_index("region")
    column_idx = lax.axis_index("rows")
    batches, obs_count = obs_order.shape
    slot_count = obs_count // group_size
    members = ensemble_state.shape[1]

    own_rows = lax.dynamic_slice_in_dim(obs_rows, column_idx * slot_count, slot_count, axis=1)
    pieces = ensemble_state[own_rows]
    pieces = pick_owner(pieces, batch_owner, "region")
    raw = lax.all_gather(pieces, "rows", axis=1, tiled=True)

    region_ids = jnp.arange(region_count, dtype=jnp.int32)
    reads = jnp.logical_or(
        region_ids[None, :] == batch_owner[:, None],
        jnp.any(readers[:, :, None] == region_ids[None, None, :], axis=1),
    )
    table = jnp.concatenate(
        [obs_values[:, :, None], obs_error[:, :, None], jnp.swapaxes(loc_taper, 1, 2)], axis=2
    )
    picks = (obs_order[:, :, None] == jnp.arange(obs_count, dtype=jnp.int32)).astype(jnp.float32)
    slot_table = jnp.einsum("bsj,bjc->bsc", picks, table, precision=lax.Precision.HIGHEST)
    slot_values = slot_table[:, :, 0]
    slot_errors = slot_table[:, :, 1]
    slot_taper = jnp.swapaxes(slot_table[:, :, 2 : 2 + region_count], 1, 2)

    pending = [(raw, k) for k in range(batches)]
    scaled_list, incr_list = [], []
    for earlier in range(batches):
        source, index = pending[earlier]
        scaled, obs_incr = adjust_rows(source, index, slot_values[earlier], slot_errors[earlier])
        scaled_list.append(scaled)
        incr_list.append(obs_incr)
        for k in range(earlier + 1, batches):
            owner = batch_owner[k]
            source, index = pending[k]
            moved = lax.cond(
                reads[earlier, owner],
                lambda rows_x, s=scaled, o=obs_incr, w=slot_taper[earlier, owner], i=index: update_rows(
                    rows_x, i, [s], [o], w[None, None, None, :], jnp.ones((1,), jnp.int32),
                    obs_count, block=512,
                ),
                lambda rows_x, i=index: rows_x[i],
                source,
            )
            pending[k] = (moved[None], 0)

    main_weights = jnp.where(reads[:, region_idx, None], slot_taper[:, region_idx], 0.0)
    current = update_rows(
        ensemble_state[None], 0, scaled_list, incr_list, main_weights[None, :, None, :],
        reads[:, region_idx], ensemble_state.shape[0], block=512,
    )
    return current


def solution(mesh):
    placed = (P(("region", "rows"), None), P(), P(), P(), P(), P(), P(), P())
    return jax.shard_map(
        local, mesh=mesh, in_specs=placed, out_specs=P(("region", "rows"), None), check_vma=False
    )
```

```python
import functools

import jax
import jax.numpy as jnp
from jax import lax
from jax.experimental import pallas as pl
from jax.experimental.pallas import tpu as pltpu
from jax.sharding import PartitionSpec as P


def adjust(prior_ens, values, errors):
    members = prior_ens.shape[1]
    prior_mean = jnp.mean(prior_ens, axis=1, keepdims=True)
    anomalies = prior_ens - prior_mean
    variance = jnp.sum(anomalies * anomalies, axis=1, keepdims=True) / (members - 1) + 1e-05
    errors = errors[:, None]
    values = values[:, None]
    post_var = variance * errors / (variance + errors)
    mean_shift = post_var * (prior_mean / variance + values / errors) - prior_mean
    shrink = jnp.sqrt(errors / (variance + errors))
    obs_incr = (mean_shift + (shrink - 1.0) * anomalies).astype(jnp.bfloat16)
    scaled = (anomalies / ((members - 1) * variance)).astype(jnp.bfloat16)
    return (scaled, obs_incr)


def adjust_kernel(prior_ref, values_ref, errors_ref, scaled_ref, incr_ref):
    prior_ens = prior_ref[...]
    members = prior_ens.shape[1]
    values = values_ref[...]
    errors = errors_ref[...]
    prior_mean = jnp.mean(prior_ens, axis=1, keepdims=True)
    anomalies = prior_ens - prior_mean
    variance = jnp.sum(anomalies * anomalies, axis=1, keepdims=True) / (members - 1) + 1e-05
    post_var = variance * errors / (variance + errors)
    mean_shift = post_var * (prior_mean / variance + values / errors) - prior_mean
    shrink = jnp.sqrt(errors / (variance + errors))
    incr_ref[...] = (mean_shift + (shrink - 1.0) * anomalies).astype(jnp.bfloat16)
    inverse = 1.0 / ((members - 1) * variance)
    scaled_ref[...] = (anomalies * inverse).astype(jnp.bfloat16)


def adjust_rows(source, index, values, errors, block=1024):
    _, rows, members = source.shape
    in_spec = pl.BlockSpec((None, block, members), lambda i: (index, i, 0))
    row_spec = pl.BlockSpec((block, members), lambda i: (i, 0))
    col_spec = pl.BlockSpec((block, 1), lambda i: (i, 0))
    out = jax.ShapeDtypeStruct((rows, members), jnp.bfloat16)
    return pl.pallas_call(
        adjust_kernel,
        grid=(rows // block,),
        in_specs=[in_spec, col_spec, col_spec],
        out_specs=[row_spec, row_spec],
        out_shape=[out, out],
    )(source, values[:, None], errors[:, None])


def update_kernel(batches, flags_ref, x_ref, *refs):
    scaled_refs = refs[:batches]
    incr_refs = refs[batches : 2 * batches]
    weights_ref = refs[2 * batches]
    out_ref = refs[2 * batches + 1]
    out_ref[...] = x_ref[...]
    for batch_idx in range(batches):

        @pl.when(flags_ref[batch_idx] != 0)
        def _(batch_idx=batch_idx):
            current = out_ref[...]
            centre = jnp.mean(current, axis=1, keepdims=True)
            state_anom = (current - centre).astype(jnp.bfloat16)
            linked = lax.dot_general(
                state_anom, scaled_refs[batch_idx][...], (((1,), (1,)), ((), ())),
                preferred_element_type=jnp.float32,
            )
            coupling = (linked * weights_ref[0, batch_idx]).astype(jnp.bfloat16)
            out_ref[...] = current + jnp.dot(
                coupling, incr_refs[batch_idx][...], preferred_element_type=jnp.float32
            )


def update_rows(source, index, scaled, obs_incr, weights, flags, group_rows, block=256):
    _, rows, members = source.shape
    batches = len(scaled)
    in_spec = pl.BlockSpec((None, block, members), lambda i, f: (index, i, 0))
    row_spec = pl.BlockSpec((block, members), lambda i, f: (i, 0))
    full_spec = pl.BlockSpec(scaled[0].shape, lambda i, f: (0, 0))
    per_group = group_rows // block
    weight_spec = pl.BlockSpec((1,) + weights.shape[1:], lambda i, f: (i // per_group, 0, 0, 0))
    return pl.pallas_call(
        functools.partial(update_kernel, batches),
        grid_spec=pltpu.PrefetchScalarGridSpec(
            num_scalar_prefetch=1,
            grid=(rows // block,),
            in_specs=[in_spec] + [full_spec] * (2 * batches) + [weight_spec],
            out_specs=row_spec,
        ),
        out_shape=jax.ShapeDtypeStruct((rows, members), source.dtype),
    )(flags.astype(jnp.int32), source, *scaled, *obs_incr, weights)


def pick_owner(pieces, owners, axis):
    size = lax.axis_size(axis)
    me = lax.axis_index(axis)
    held = pieces
    step = 1
    while step < size:
        partner = lax.ppermute(held, axis, [(i, i ^ step) for i in range(size)])
        keep = ((me // step) % 2) == ((owners // step) % 2)
        held = jnp.where(keep[:, None, None], held, partner)
        step *= 2
    return held


def gather_rows(pieces, axis, dims=(4, 4, 2)):
    ny, nx, nc = dims
    size = lax.axis_size(axis)
    me = lax.axis_index(axis)
    width = pieces.shape[1]
    held = jnp.zeros(pieces.shape[:1] + (size * width,) + pieces.shape[2:], pieces.dtype)
    held = lax.dynamic_update_slice_in_dim(held, pieces, me * width, axis=1)
    coords = [(c // (nx * nc), (c // nc) % nx, c % nc) for c in range(size)]

    def index(y, x, core):
        return (y % ny) * nx * nc + (x % nx) * nc + core

    def shifted(dy, dx, dcore):
        return [(c, index(y + dy, x + dx, (core + dcore) % nc)) for c, (y, x, core) in enumerate(coords)]

    my_y, my_x = me // (nx * nc), (me // nc) % nx
    theirs = lax.ppermute(pieces, axis, shifted(0, 0, 1))
    held = lax.dynamic_update_slice_in_dim(held, theirs, (me ^ 1) * width, axis=1)

    def ring(held, block, span, lane, offset_of):
        from_minus = lax.ppermute(block, axis, lane(1))
        from_plus = lax.ppermute(block, axis, lane(-1))
        held = lax.dynamic_update_slice_in_dim(held, from_minus, offset_of(-1), axis=1)
        held = lax.dynamic_update_slice_in_dim(held, from_plus, offset_of(1), axis=1)
        from_two = lax.ppermute(from_minus, axis, lane(1))
        return lax.dynamic_update_slice_in_dim(held, from_two, offset_of(-2), axis=1)

    chip = nc * width
    block = lax.dynamic_slice_in_dim(held, (me // nc) * chip, chip, axis=1)
    held = ring(
        held, block, chip, lambda d: shifted(0, d, 0),
        lambda k: (my_y * nx + (my_x + k) % nx) * chip,
    )
    line = nx * chip
    block = lax.dynamic_slice_in_dim(held, my_y * line, line, axis=1)
    held = ring(held, block, line, lambda d: shifted(d, 0, 0), lambda k: ((my_y + k) % ny) * line)
    return held


def local(
    ensemble_state, obs_values, obs_error, batch_owner, readers, obs_order, obs_rows, loc_taper
):
    group_size = lax.axis_size("rows")
    region_count = lax.axis_size("region")
    region_idx = lax.axis_index("region")
    column_idx = lax.axis_index("rows")
    batches, obs_count = obs_order.shape
    slot_count = obs_count // group_size
    members = ensemble_state.shape[1]

    own_rows = lax.dynamic_slice_in_dim(obs_rows, column_idx * slot_count, slot_count, axis=1)
    pieces = ensemble_state[own_rows]
    pieces = pick_owner(pieces, batch_owner, "region")
    raw = gather_rows(pieces, "rows")

    region_ids = jnp.arange(region_count, dtype=jnp.int32)
    reads = jnp.logical_or(
        region_ids[None, :] == batch_owner[:, None],
        jnp.any(readers[:, :, None] == region_ids[None, None, :], axis=1),
    )
    table = jnp.concatenate(
        [obs_values[:, :, None], obs_error[:, :, None], jnp.swapaxes(loc_taper, 1, 2)], axis=2
    )
    picks = (obs_order[:, :, None] == jnp.arange(obs_count, dtype=jnp.int32)).astype(jnp.float32)
    slot_table = jnp.einsum("bsj,bjc->bsc", picks, table, precision=lax.Precision.HIGHEST)
    slot_values = slot_table[:, :, 0]
    slot_errors = slot_table[:, :, 1]
    slot_taper = jnp.swapaxes(slot_table[:, :, 2 : 2 + region_count], 1, 2)

    pending = [(raw, k) for k in range(batches)]
    scaled_list, incr_list = [], []
    for earlier in range(batches):
        source, index = pending[earlier]
        scaled, obs_incr = adjust_rows(source, index, slot_values[earlier], slot_errors[earlier])
        scaled_list.append(scaled)
        incr_list.append(obs_incr)
        for k in range(earlier + 1, batches):
            owner = batch_owner[k]
            source, index = pending[k]
            moved = lax.cond(
                reads[earlier, owner],
                lambda rows_x, s=scaled, o=obs_incr, w=slot_taper[earlier, owner], i=index: update_rows(
                    rows_x, i, [s], [o], w[None, None, None, :], jnp.ones((1,), jnp.int32),
                    obs_count, block=512,
                ),
                lambda rows_x, i=index: rows_x[i],
                source,
            )
            pending[k] = (moved[None], 0)

    main_weights = jnp.where(reads[:, region_idx, None], slot_taper[:, region_idx], 0.0)
    current = update_rows(
        ensemble_state[None], 0, scaled_list, incr_list, main_weights[None, :, None, :],
        reads[:, region_idx], ensemble_state.shape[0], block=512,
    )
    return current


def solution(mesh):
    placed = (P(("region", "rows"), None), P(), P(), P(), P(), P(), P(), P())
    return jax.shard_map(
        local, mesh=mesh, in_specs=placed, out_specs=P(("region", "rows"), None), check_vma=False
    )
```

```python
import functools

import jax
import jax.numpy as jnp
from jax import lax
from jax.experimental import pallas as pl
from jax.experimental.pallas import tpu as pltpu
from jax.sharding import PartitionSpec as P


def adjust(prior_ens, values, errors):
    members = prior_ens.shape[1]
    prior_mean = jnp.mean(prior_ens, axis=1, keepdims=True)
    anomalies = prior_ens - prior_mean
    variance = jnp.sum(anomalies * anomalies, axis=1, keepdims=True) / (members - 1) + 1e-05
    errors = errors[:, None]
    values = values[:, None]
    post_var = variance * errors / (variance + errors)
    mean_shift = post_var * (prior_mean / variance + values / errors) - prior_mean
    shrink = jnp.sqrt(errors / (variance + errors))
    obs_incr = (mean_shift + (shrink - 1.0) * anomalies).astype(jnp.bfloat16)
    scaled = (anomalies / ((members - 1) * variance)).astype(jnp.bfloat16)
    return (scaled, obs_incr)


def adjust_kernel(prior_ref, table_ref, scaled_ref, incr_ref):
    prior_ens = prior_ref[...]
    members = prior_ens.shape[1]
    table = table_ref[...]
    values = table[:, 0:1]
    errors = table[:, 1:2]
    prior_mean = jnp.mean(prior_ens, axis=1, keepdims=True)
    anomalies = prior_ens - prior_mean
    variance = jnp.sum(anomalies * anomalies, axis=1, keepdims=True) / (members - 1) + 1e-05
    post_var = variance * errors / (variance + errors)
    mean_shift = post_var * (prior_mean / variance + values / errors) - prior_mean
    shrink = jnp.sqrt(errors / (variance + errors))
    incr_ref[...] = (mean_shift + (shrink - 1.0) * anomalies).astype(jnp.bfloat16)
    inverse = 1.0 / ((members - 1) * variance)
    scaled_ref[...] = (anomalies * inverse).astype(jnp.bfloat16)


def adjust_rows(source, index, table, batch, block=1024):
    _, rows, members = source.shape
    in_spec = pl.BlockSpec((None, block, members), lambda i: (index, i, 0))
    table_spec = pl.BlockSpec((None, block, table.shape[2]), lambda i: (batch, i, 0))
    row_spec = pl.BlockSpec((block, members), lambda i: (i, 0))
    out = jax.ShapeDtypeStruct((rows, members), jnp.bfloat16)
    return pl.pallas_call(
        adjust_kernel,
        grid=(rows // block,),
        in_specs=[in_spec, table_spec],
        out_specs=[row_spec, row_spec],
        out_shape=[out, out],
    )(source, table)


def update_kernel(batches, flags_ref, x_ref, *refs):
    scaled_refs = refs[:batches]
    incr_refs = refs[batches : 2 * batches]
    weights_ref = refs[2 * batches]
    out_ref = refs[2 * batches + 1]
    out_ref[...] = x_ref[...]
    for batch_idx in range(batches):

        @pl.when(flags_ref[batch_idx] != 0)
        def _(batch_idx=batch_idx):
            current = out_ref[...]
            centre = jnp.mean(current, axis=1, keepdims=True)
            state_anom = (current - centre).astype(jnp.bfloat16)
            linked = lax.dot_general(
                state_anom, scaled_refs[batch_idx][...], (((1,), (1,)), ((), ())),
                preferred_element_type=jnp.float32,
            )
            coupling = (linked * weights_ref[0, batch_idx]).astype(jnp.bfloat16)
            out_ref[...] = current + jnp.dot(
                coupling, incr_refs[batch_idx][...], preferred_element_type=jnp.float32
            )


def update_rows(source, index, scaled, obs_incr, weights, flags, group_rows, block=256):
    _, rows, members = source.shape
    batches = len(scaled)
    in_spec = pl.BlockSpec((None, block, members), lambda i, f: (index, i, 0))
    row_spec = pl.BlockSpec((block, members), lambda i, f: (i, 0))
    full_spec = pl.BlockSpec(scaled[0].shape, lambda i, f: (0, 0))
    per_group = group_rows // block
    weight_spec = pl.BlockSpec((1,) + weights.shape[1:], lambda i, f: (i // per_group, 0, 0, 0))
    return pl.pallas_call(
        functools.partial(update_kernel, batches),
        grid_spec=pltpu.PrefetchScalarGridSpec(
            num_scalar_prefetch=1,
            grid=(rows // block,),
            in_specs=[in_spec] + [full_spec] * (2 * batches) + [weight_spec],
            out_specs=row_spec,
        ),
        out_shape=jax.ShapeDtypeStruct((rows, members), source.dtype),
    )(flags.astype(jnp.int32), source, *scaled, *obs_incr, weights)


def pick_owner(pieces, owners, axis):
    size = lax.axis_size(axis)
    me = lax.axis_index(axis)
    held = pieces
    step = 1
    while step < size:
        partner = lax.ppermute(held, axis, [(i, i ^ step) for i in range(size)])
        keep = ((me // step) % 2) == ((owners // step) % 2)
        held = jnp.where(keep[:, None, None], held, partner)
        step *= 2
    return held


def gather_rows(pieces, axis, dims=(4, 4, 2)):
    ny, nx, nc = dims
    size = lax.axis_size(axis)
    me = lax.axis_index(axis)
    width = pieces.shape[1]
    held = jnp.zeros(pieces.shape[:1] + (size * width,) + pieces.shape[2:], pieces.dtype)
    held = lax.dynamic_update_slice_in_dim(held, pieces, me * width, axis=1)
    coords = [(c // (nx * nc), (c // nc) % nx, c % nc) for c in range(size)]

    def index(y, x, core):
        return (y % ny) * nx * nc + (x % nx) * nc + core

    def shifted(dy, dx, dcore):
        return [(c, index(y + dy, x + dx, (core + dcore) % nc)) for c, (y, x, core) in enumerate(coords)]

    my_y, my_x = me // (nx * nc), (me // nc) % nx
    theirs = lax.ppermute(pieces, axis, shifted(0, 0, 1))
    held = lax.dynamic_update_slice_in_dim(held, theirs, (me ^ 1) * width, axis=1)

    def ring(held, block, span, lane, offset_of):
        from_minus = lax.ppermute(block, axis, lane(1))
        from_plus = lax.ppermute(block, axis, lane(-1))
        held = lax.dynamic_update_slice_in_dim(held, from_minus, offset_of(-1), axis=1)
        held = lax.dynamic_update_slice_in_dim(held, from_plus, offset_of(1), axis=1)
        from_two = lax.ppermute(from_minus, axis, lane(1))
        return lax.dynamic_update_slice_in_dim(held, from_two, offset_of(-2), axis=1)

    chip = nc * width
    block = lax.dynamic_slice_in_dim(held, (me // nc) * chip, chip, axis=1)
    held = ring(
        held, block, chip, lambda d: shifted(0, d, 0),
        lambda k: (my_y * nx + (my_x + k) % nx) * chip,
    )
    line = nx * chip
    block = lax.dynamic_slice_in_dim(held, my_y * line, line, axis=1)
    held = ring(held, block, line, lambda d: shifted(d, 0, 0), lambda k: ((my_y + k) % ny) * line)
    return held


def local(
    ensemble_state, obs_values, obs_error, batch_owner, readers, obs_order, obs_rows, loc_taper
):
    group_size = lax.axis_size("rows")
    region_count = lax.axis_size("region")
    region_idx = lax.axis_index("region")
    column_idx = lax.axis_index("rows")
    batches, obs_count = obs_order.shape
    slot_count = obs_count // group_size
    members = ensemble_state.shape[1]

    own_rows = lax.dynamic_slice_in_dim(obs_rows, column_idx * slot_count, slot_count, axis=1)
    pieces = ensemble_state[own_rows]
    pieces = pick_owner(pieces, batch_owner, "region")
    raw = gather_rows(pieces, "rows")

    region_ids = jnp.arange(region_count, dtype=jnp.int32)
    reads = jnp.logical_or(
        region_ids[None, :] == batch_owner[:, None],
        jnp.any(readers[:, :, None] == region_ids[None, None, :], axis=1),
    )
    table = jnp.concatenate(
        [obs_values[:, :, None], obs_error[:, :, None], jnp.swapaxes(loc_taper, 1, 2)], axis=2
    )
    picks = (obs_order[:, :, None] == jnp.arange(obs_count, dtype=jnp.int32)).astype(jnp.float32)
    slot_table = jnp.einsum("bsj,bjc->bsc", picks, table, precision=lax.Precision.HIGHEST)
    slot_taper = jnp.swapaxes(slot_table[:, :, 2 : 2 + region_count], 1, 2)

    pending = [(raw, k) for k in range(batches)]
    scaled_list, incr_list = [], []
    for earlier in range(batches):
        source, index = pending[earlier]
        scaled, obs_incr = adjust_rows(source, index, slot_table, earlier)
        scaled_list.append(scaled)
        incr_list.append(obs_incr)
        for k in range(earlier + 1, batches):
            owner = batch_owner[k]
            source, index = pending[k]
            moved = lax.cond(
                reads[earlier, owner],
                lambda rows_x, s=scaled, o=obs_incr, w=slot_taper[earlier, owner], i=index: update_rows(
                    rows_x, i, [s], [o], w[None, None, None, :], jnp.ones((1,), jnp.int32),
                    obs_count, block=512,
                ),
                lambda rows_x, i=index: rows_x[i],
                source,
            )
            pending[k] = (moved[None], 0)

    main_weights = jnp.where(reads[:, region_idx, None], slot_taper[:, region_idx], 0.0)
    current = update_rows(
        ensemble_state[None], 0, scaled_list, incr_list, main_weights[None, :, None, :],
        reads[:, region_idx], ensemble_state.shape[0], block=512,
    )
    return current


def solution(mesh):
    placed = (P(("region", "rows"), None), P(), P(), P(), P(), P(), P(), P())
    return jax.shard_map(
        local, mesh=mesh, in_specs=placed, out_specs=P(("region", "rows"), None), check_vma=False
    )
```

```python
import functools

import jax
import jax.numpy as jnp
from jax import lax
from jax.experimental import pallas as pl
from jax.experimental.pallas import tpu as pltpu
from jax.sharding import PartitionSpec as P


def adjust(prior_ens, values, errors):
    members = prior_ens.shape[1]
    prior_mean = jnp.mean(prior_ens, axis=1, keepdims=True)
    anomalies = prior_ens - prior_mean
    variance = jnp.sum(anomalies * anomalies, axis=1, keepdims=True) / (members - 1) + 1e-05
    errors = errors[:, None]
    values = values[:, None]
    post_var = variance * errors / (variance + errors)
    mean_shift = post_var * (prior_mean / variance + values / errors) - prior_mean
    shrink = jnp.sqrt(errors / (variance + errors))
    obs_incr = (mean_shift + (shrink - 1.0) * anomalies).astype(jnp.bfloat16)
    scaled = (anomalies / ((members - 1) * variance)).astype(jnp.bfloat16)
    return (scaled, obs_incr)


def adjust_kernel(prior_ref, table_ref, scaled_ref, incr_ref):
    prior_ens = prior_ref[...]
    members = prior_ens.shape[1]
    table = table_ref[...]
    values = table[:, 0:1]
    errors = table[:, 1:2]
    prior_mean = jnp.mean(prior_ens, axis=1, keepdims=True)
    anomalies = prior_ens - prior_mean
    variance = jnp.sum(anomalies * anomalies, axis=1, keepdims=True) / (members - 1) + 1e-05
    post_var = variance * errors / (variance + errors)
    mean_shift = post_var * (prior_mean / variance + values / errors) - prior_mean
    shrink = jnp.sqrt(errors / (variance + errors))
    incr_ref[...] = (mean_shift + (shrink - 1.0) * anomalies).astype(jnp.bfloat16)
    inverse = 1.0 / ((members - 1) * variance)
    scaled_ref[...] = (anomalies * inverse).astype(jnp.bfloat16)


def adjust_rows(source, index, table, batch, block=1024):
    _, rows, members = source.shape
    in_spec = pl.BlockSpec((None, block, members), lambda i: (index, i, 0))
    table_spec = pl.BlockSpec((None, block, table.shape[2]), lambda i: (batch, i, 0))
    row_spec = pl.BlockSpec((block, members), lambda i: (i, 0))
    out = jax.ShapeDtypeStruct((rows, members), jnp.bfloat16)
    return pl.pallas_call(
        adjust_kernel,
        grid=(rows // block,),
        in_specs=[in_spec, table_spec],
        out_specs=[row_spec, row_spec],
        out_shape=[out, out],
    )(source, table)


def update_kernel(batches, flags_ref, x_ref, *refs):
    scaled_refs = refs[:batches]
    incr_refs = refs[batches : 2 * batches]
    weights_ref = refs[2 * batches]
    out_ref = refs[2 * batches + 1]
    out_ref[...] = x_ref[...]
    for batch_idx in range(batches):

        @pl.when(flags_ref[batch_idx] != 0)
        def _(batch_idx=batch_idx):
            current = out_ref[...]
            centre = jnp.mean(current, axis=1, keepdims=True)
            state_anom = (current - centre).astype(jnp.bfloat16)
            linked = lax.dot_general(
                state_anom, scaled_refs[batch_idx][...], (((1,), (1,)), ((), ())),
                preferred_element_type=jnp.float32,
            )
            coupling = (linked * weights_ref[0, batch_idx]).astype(jnp.bfloat16)
            out_ref[...] = current + jnp.dot(
                coupling, incr_refs[batch_idx][...], preferred_element_type=jnp.float32
            )


def update_rows(source, index, scaled, obs_incr, weights, flags, group_rows, block=256):
    _, rows, members = source.shape
    batches = len(scaled)
    in_spec = pl.BlockSpec((None, block, members), lambda i, f: (index, i, 0))
    row_spec = pl.BlockSpec((block, members), lambda i, f: (i, 0))
    full_spec = pl.BlockSpec(scaled[0].shape, lambda i, f: (0, 0))
    per_group = group_rows // block
    weight_spec = pl.BlockSpec((1,) + weights.shape[1:], lambda i, f: (i // per_group, 0, 0, 0))
    return pl.pallas_call(
        functools.partial(update_kernel, batches),
        grid_spec=pltpu.PrefetchScalarGridSpec(
            num_scalar_prefetch=1,
            grid=(rows // block,),
            in_specs=[in_spec] + [full_spec] * (2 * batches) + [weight_spec],
            out_specs=row_spec,
        ),
        out_shape=jax.ShapeDtypeStruct((rows, members), source.dtype),
    )(flags.astype(jnp.int32), source, *scaled, *obs_incr, weights)


def pick_owner(pieces, owners, axis):
    size = lax.axis_size(axis)
    me = lax.axis_index(axis)
    held = pieces
    step = 1
    while step < size:
        partner = lax.ppermute(held, axis, [(i, i ^ step) for i in range(size)])
        keep = ((me // step) % 2) == ((owners // step) % 2)
        held = jnp.where(keep[:, None, None], held, partner)
        step *= 2
    return held


def gather_rows(pieces, axis, side, dims=(4, 4, 2)):
    ny, nx, nc = dims
    size = lax.axis_size(axis)
    me = lax.axis_index(axis)
    width = pieces.shape[1]
    held = jnp.zeros(pieces.shape[:1] + (size * width,) + pieces.shape[2:], pieces.dtype)
    held = lax.dynamic_update_slice_in_dim(held, pieces, me * width, axis=1)
    coords = [(c // (nx * nc), (c // nc) % nx, c % nc) for c in range(size)]

    def index(y, x, core):
        return (y % ny) * nx * nc + (x % nx) * nc + core

    def shifted(dy, dx, dcore):
        return [(c, index(y + dy, x + dx, (core + dcore) % nc)) for c, (y, x, core) in enumerate(coords)]

    my_y, my_x = me // (nx * nc), (me // nc) % nx
    theirs = lax.ppermute(pieces, axis, shifted(0, 0, 1))
    held = lax.dynamic_update_slice_in_dim(held, theirs, (me ^ 1) * width, axis=1)

    def ring(held, block, span, lane, offset_of, side=None):
        from_minus = lax.ppermute(block, axis, lane(1))
        from_plus = lax.ppermute(block, axis, lane(-1))
        if side is not None:
            from_minus, side = lax.optimization_barrier((from_minus, side))
        held = lax.dynamic_update_slice_in_dim(held, from_minus, offset_of(-1), axis=1)
        held = lax.dynamic_update_slice_in_dim(held, from_plus, offset_of(1), axis=1)
        from_two = lax.ppermute(from_minus, axis, lane(1))
        return lax.dynamic_update_slice_in_dim(held, from_two, offset_of(-2), axis=1), side

    chip = nc * width
    block = lax.dynamic_slice_in_dim(held, (me // nc) * chip, chip, axis=1)
    held, _ = ring(
        held, block, chip, lambda d: shifted(0, d, 0),
        lambda k: (my_y * nx + (my_x + k) % nx) * chip,
    )
    line = nx * chip
    block = lax.dynamic_slice_in_dim(held, my_y * line, line, axis=1)
    held, side = ring(
        held, block, line, lambda d: shifted(d, 0, 0), lambda k: ((my_y + k) % ny) * line, side
    )
    return held, side


def local(
    ensemble_state, obs_values, obs_error, batch_owner, readers, obs_order, obs_rows, loc_taper
):
    group_size = lax.axis_size("rows")
    region_count = lax.axis_size("region")
    region_idx = lax.axis_index("region")
    column_idx = lax.axis_index("rows")
    batches, obs_count = obs_order.shape
    slot_count = obs_count // group_size
    members = ensemble_state.shape[1]

    own_rows = lax.dynamic_slice_in_dim(obs_rows, column_idx * slot_count, slot_count, axis=1)
    pieces = ensemble_state[own_rows]
    pieces = pick_owner(pieces, batch_owner, "region")

    region_ids = jnp.arange(region_count, dtype=jnp.int32)
    reads = jnp.logical_or(
        region_ids[None, :] == batch_owner[:, None],
        jnp.any(readers[:, :, None] == region_ids[None, None, :], axis=1),
    )
    table = jnp.concatenate(
        [obs_values[:, :, None], obs_error[:, :, None], jnp.swapaxes(loc_taper, 1, 2)], axis=2
    )
    picks = (obs_order[:, :, None] == jnp.arange(obs_count, dtype=jnp.int32)).astype(jnp.float32)
    slot_table = jnp.einsum("bsj,bjc->bsc", picks, table, precision=lax.Precision.HIGHEST)
    slot_taper = jnp.swapaxes(slot_table[:, :, 2 : 2 + region_count], 1, 2)

    main_weights = jnp.where(reads[:, region_idx, None], slot_taper[:, region_idx], 0.0)
    raw, (slot_table, slot_taper, main_weights) = gather_rows(
        pieces, "rows", (slot_table, slot_taper, main_weights)
    )

    pending = [(raw, k) for k in range(batches)]
    scaled_list, incr_list = [], []
    for earlier in range(batches):
        source, index = pending[earlier]
        scaled, obs_incr = adjust_rows(source, index, slot_table, earlier)
        scaled_list.append(scaled)
        incr_list.append(obs_incr)
        for k in range(earlier + 1, batches):
            owner = batch_owner[k]
            source, index = pending[k]
            moved = lax.cond(
                reads[earlier, owner],
                lambda rows_x, s=scaled, o=obs_incr, w=slot_taper[earlier, owner], i=index: update_rows(
                    rows_x, i, [s], [o], w[None, None, None, :], jnp.ones((1,), jnp.int32),
                    obs_count, block=512,
                ),
                lambda rows_x, i=index: rows_x[i],
                source,
            )
            pending[k] = (moved[None], 0)

    current = update_rows(
        ensemble_state[None], 0, scaled_list, incr_list, main_weights[None, :, None, :],
        reads[:, region_idx], ensemble_state.shape[0], block=512,
    )
    return current


def solution(mesh):
    placed = (P(("region", "rows"), None), P(), P(), P(), P(), P(), P(), P())
    return jax.shard_map(
        local, mesh=mesh, in_specs=placed, out_specs=P(("region", "rows"), None), check_vma=False
    )
```

```python
import functools

import jax
import jax.numpy as jnp
from jax import lax
from jax.experimental import pallas as pl
from jax.experimental.pallas import tpu as pltpu
from jax.sharding import PartitionSpec as P


def adjust(prior_ens, values, errors):
    members = prior_ens.shape[1]
    prior_mean = jnp.mean(prior_ens, axis=1, keepdims=True)
    anomalies = prior_ens - prior_mean
    variance = jnp.sum(anomalies * anomalies, axis=1, keepdims=True) / (members - 1) + 1e-05
    errors = errors[:, None]
    values = values[:, None]
    post_var = variance * errors / (variance + errors)
    mean_shift = post_var * (prior_mean / variance + values / errors) - prior_mean
    shrink = jnp.sqrt(errors / (variance + errors))
    obs_incr = (mean_shift + (shrink - 1.0) * anomalies).astype(jnp.bfloat16)
    scaled = (anomalies / ((members - 1) * variance)).astype(jnp.bfloat16)
    return (scaled, obs_incr)


def adjust_kernel(prior_ref, values_ref, errors_ref, scaled_ref, incr_ref):
    prior_ens = prior_ref[...]
    members = prior_ens.shape[1]
    values = values_ref[...]
    errors = errors_ref[...]
    prior_mean = jnp.mean(prior_ens, axis=1, keepdims=True)
    anomalies = prior_ens - prior_mean
    variance = jnp.sum(anomalies * anomalies, axis=1, keepdims=True) / (members - 1) + 1e-05
    post_var = variance * errors / (variance + errors)
    mean_shift = post_var * (prior_mean / variance + values / errors) - prior_mean
    shrink = jnp.sqrt(errors / (variance + errors))
    incr_ref[...] = (mean_shift + (shrink - 1.0) * anomalies).astype(jnp.bfloat16)
    inverse = 1.0 / ((members - 1) * variance)
    scaled_ref[...] = (anomalies * inverse).astype(jnp.bfloat16)


def adjust_rows(source, index, values, errors, block=512):
    _, rows, members = source.shape
    in_spec = pl.BlockSpec((None, block, members), lambda i: (index, i, 0))
    row_spec = pl.BlockSpec((block, members), lambda i: (i, 0))
    col_spec = pl.BlockSpec((block, 1), lambda i: (i, 0))
    out = jax.ShapeDtypeStruct((rows, members), jnp.bfloat16)
    return pl.pallas_call(
        adjust_kernel,
        grid=(rows // block,),
        in_specs=[in_spec, col_spec, col_spec],
        out_specs=[row_spec, row_spec],
        out_shape=[out, out],
    )(source, values[:, None], errors[:, None])


def update_kernel(batches, flags_ref, x_ref, *refs):
    scaled_refs = refs[:batches]
    incr_refs = refs[batches : 2 * batches]
    weights_ref = refs[2 * batches]
    out_ref = refs[2 * batches + 1]
    out_ref[...] = x_ref[...]
    for batch_idx in range(batches):

        @pl.when(flags_ref[batch_idx] != 0)
        def _(batch_idx=batch_idx):
            current = out_ref[...]
            centre = jnp.mean(current, axis=1, keepdims=True)
            state_anom = (current - centre).astype(jnp.bfloat16)
            linked = lax.dot_general(
                state_anom, scaled_refs[batch_idx][...], (((1,), (1,)), ((), ())),
                preferred_element_type=jnp.float32,
            )
            coupling = (linked * weights_ref[0, batch_idx]).astype(jnp.bfloat16)
            out_ref[...] = current + jnp.dot(
                coupling, incr_refs[batch_idx][...], preferred_element_type=jnp.float32
            )


def update_rows(source, index, scaled, obs_incr, weights, flags, group_rows, block=256):
    _, rows, members = source.shape
    batches = len(scaled)
    in_spec = pl.BlockSpec((None, block, members), lambda i, f: (index, i, 0))
    row_spec = pl.BlockSpec((block, members), lambda i, f: (i, 0))
    full_spec = pl.BlockSpec(scaled[0].shape, lambda i, f: (0, 0))
    per_group = group_rows // block
    weight_spec = pl.BlockSpec((1,) + weights.shape[1:], lambda i, f: (i // per_group, 0, 0, 0))
    return pl.pallas_call(
        functools.partial(update_kernel, batches),
        grid_spec=pltpu.PrefetchScalarGridSpec(
            num_scalar_prefetch=1,
            grid=(rows // block,),
            in_specs=[in_spec] + [full_spec] * (2 * batches) + [weight_spec],
            out_specs=row_spec,
        ),
        out_shape=jax.ShapeDtypeStruct((rows, members), source.dtype),
    )(flags.astype(jnp.int32), source, *scaled, *obs_incr, weights)


def pick_owner(pieces, owners, axis):
    size = lax.axis_size(axis)
    me = lax.axis_index(axis)
    held = pieces
    step = 1
    while step < size:
        partner = lax.ppermute(held, axis, [(i, i ^ step) for i in range(size)])
        keep = ((me // step) % 2) == ((owners // step) % 2)
        held = jnp.where(keep[:, None, None], held, partner)
        step *= 2
    return held


def local(
    ensemble_state, obs_values, obs_error, batch_owner, readers, obs_order, obs_rows, loc_taper
):
    group_size = lax.axis_size("rows")
    region_count = lax.axis_size("region")
    region_idx = lax.axis_index("region")
    column_idx = lax.axis_index("rows")
    batches, obs_count = obs_order.shape
    slot_count = obs_count // group_size
    members = ensemble_state.shape[1]

    own_rows = lax.dynamic_slice_in_dim(obs_rows, column_idx * slot_count, slot_count, axis=1)
    pieces = ensemble_state[own_rows]
    pieces = pick_owner(pieces, batch_owner, "region")
    raw = lax.all_gather(pieces, "rows", axis=1, tiled=True)

    region_ids = jnp.arange(region_count, dtype=jnp.int32)
    reads = jnp.logical_or(
        region_ids[None, :] == batch_owner[:, None],
        jnp.any(readers[:, :, None] == region_ids[None, None, :], axis=1),
    )
    table = jnp.concatenate(
        [obs_values[:, :, None], obs_error[:, :, None], jnp.swapaxes(loc_taper, 1, 2)], axis=2
    )
    picks = (obs_order[:, :, None] == jnp.arange(obs_count, dtype=jnp.int32)).astype(jnp.float32)
    slot_table = jnp.einsum("bsj,bjc->bsc", picks, table, precision=lax.Precision.HIGHEST)
    slot_values = slot_table[:, :, 0]
    slot_errors = slot_table[:, :, 1]
    slot_taper = jnp.swapaxes(slot_table[:, :, 2 : 2 + region_count], 1, 2)

    pending = [(raw, k) for k in range(batches)]
    scaled_list, incr_list = [], []
    for earlier in range(batches):
        source, index = pending[earlier]
        scaled, obs_incr = adjust_rows(source, index, slot_values[earlier], slot_errors[earlier])
        scaled_list.append(scaled)
        incr_list.append(obs_incr)
        for k in range(earlier + 1, batches):
            owner = batch_owner[k]
            source, index = pending[k]
            applies = reads[earlier, owner]
            weights = jnp.where(applies, slot_taper[earlier, owner], 0.0)
            moved = update_rows(
                source, index, [scaled], [obs_incr], weights[None, None, None, :], applies[None],
                obs_count, block=512,
            )
            pending[k] = (moved[None], 0)

    main_weights = jnp.where(reads[:, region_idx, None], slot_taper[:, region_idx], 0.0)
    current = update_rows(
        ensemble_state[None], 0, scaled_list, incr_list, main_weights[None, :, None, :],
        reads[:, region_idx], ensemble_state.shape[0],
    )
    return current


def solution(mesh):
    placed = (P(("region", "rows"), None), P(), P(), P(), P(), P(), P(), P())
    return jax.shard_map(
        local, mesh=mesh, in_specs=placed, out_specs=P(("region", "rows"), None), check_vma=False
    )
```

```python
import functools

import jax
import jax.numpy as jnp
from jax import lax
from jax.experimental import pallas as pl
from jax.experimental.pallas import tpu as pltpu
from jax.sharding import PartitionSpec as P


def adjust(prior_ens, values, errors):
    members = prior_ens.shape[1]
    prior_mean = jnp.mean(prior_ens, axis=1, keepdims=True)
    anomalies = prior_ens - prior_mean
    variance = jnp.sum(anomalies * anomalies, axis=1, keepdims=True) / (members - 1) + 1e-05
    errors = errors[:, None]
    values = values[:, None]
    post_var = variance * errors / (variance + errors)
    mean_shift = post_var * (prior_mean / variance + values / errors) - prior_mean
    shrink = jnp.sqrt(errors / (variance + errors))
    obs_incr = (mean_shift + (shrink - 1.0) * anomalies).astype(jnp.bfloat16)
    scaled = (anomalies / ((members - 1) * variance)).astype(jnp.bfloat16)
    return (scaled, obs_incr)


def adjust_kernel(prior_ref, values_ref, errors_ref, scaled_ref, incr_ref):
    prior_ens = prior_ref[...]
    members = prior_ens.shape[1]
    values = values_ref[...]
    errors = errors_ref[...]
    prior_mean = jnp.mean(prior_ens, axis=1, keepdims=True)
    anomalies = prior_ens - prior_mean
    variance = jnp.sum(anomalies * anomalies, axis=1, keepdims=True) / (members - 1) + 1e-05
    blend = 1.0 / (variance + errors)
    post_var = variance * errors * blend
    mean_shift = post_var * (prior_mean / variance + values / errors) - prior_mean
    shrink = jnp.sqrt(errors * blend)
    incr_ref[...] = (mean_shift + (shrink - 1.0) * anomalies).astype(jnp.bfloat16)
    inverse = 1.0 / ((members - 1) * variance)
    scaled_ref[...] = (anomalies * inverse).astype(jnp.bfloat16)


def adjust_rows(source, index, values, errors, block=512):
    _, rows, members = source.shape
    in_spec = pl.BlockSpec((None, block, members), lambda i: (index, i, 0))
    row_spec = pl.BlockSpec((block, members), lambda i: (i, 0))
    col_spec = pl.BlockSpec((block, 1), lambda i: (i, 0))
    out = jax.ShapeDtypeStruct((rows, members), jnp.bfloat16)
    return pl.pallas_call(
        adjust_kernel,
        grid=(rows // block,),
        in_specs=[in_spec, col_spec, col_spec],
        out_specs=[row_spec, row_spec],
        out_shape=[out, out],
    )(source, values[:, None], errors[:, None])


def update_kernel(batches, flags_ref, x_ref, *refs):
    scaled_refs = refs[:batches]
    incr_refs = refs[batches : 2 * batches]
    weights_ref = refs[2 * batches]
    out_ref = refs[2 * batches + 1]
    out_ref[...] = x_ref[...]
    for batch_idx in range(batches):

        @pl.when(flags_ref[batch_idx] != 0)
        def _(batch_idx=batch_idx):
            current = out_ref[...]
            centre = jnp.mean(current, axis=1, keepdims=True)
            state_anom = (current - centre).astype(jnp.bfloat16)
            linked = lax.dot_general(
                state_anom, scaled_refs[batch_idx][...], (((1,), (1,)), ((), ())),
                preferred_element_type=jnp.float32,
            )
            coupling = (linked * weights_ref[0, batch_idx]).astype(jnp.bfloat16)
            out_ref[...] = current + jnp.dot(
                coupling, incr_refs[batch_idx][...], preferred_element_type=jnp.float32
            )


def update_rows(source, index, scaled, obs_incr, weights, flags, group_rows, block=256):
    _, rows, members = source.shape
    batches = len(scaled)
    in_spec = pl.BlockSpec((None, block, members), lambda i, f: (index, i, 0))
    row_spec = pl.BlockSpec((block, members), lambda i, f: (i, 0))
    full_spec = pl.BlockSpec(scaled[0].shape, lambda i, f: (0, 0))
    per_group = group_rows // block
    weight_spec = pl.BlockSpec((1,) + weights.shape[1:], lambda i, f: (i // per_group, 0, 0, 0))
    return pl.pallas_call(
        functools.partial(update_kernel, batches),
        grid_spec=pltpu.PrefetchScalarGridSpec(
            num_scalar_prefetch=1,
            grid=(rows // block,),
            in_specs=[in_spec] + [full_spec] * (2 * batches) + [weight_spec],
            out_specs=row_spec,
        ),
        out_shape=jax.ShapeDtypeStruct((rows, members), source.dtype),
    )(flags.astype(jnp.int32), source, *scaled, *obs_incr, weights)


def pick_owner(pieces, owners, axis):
    size = lax.axis_size(axis)
    me = lax.axis_index(axis)
    held = pieces
    step = 1
    while step < size:
        partner = lax.ppermute(held, axis, [(i, i ^ step) for i in range(size)])
        keep = ((me // step) % 2) == ((owners // step) % 2)
        held = jnp.where(keep[:, None, None], held, partner)
        step *= 2
    return held


def local(
    ensemble_state, obs_values, obs_error, batch_owner, readers, obs_order, obs_rows, loc_taper
):
    group_size = lax.axis_size("rows")
    region_count = lax.axis_size("region")
    region_idx = lax.axis_index("region")
    column_idx = lax.axis_index("rows")
    batches, obs_count = obs_order.shape
    slot_count = obs_count // group_size
    members = ensemble_state.shape[1]

    own_rows = lax.dynamic_slice_in_dim(obs_rows, column_idx * slot_count, slot_count, axis=1)
    pieces = ensemble_state[own_rows]
    pieces = pick_owner(pieces, batch_owner, "region")
    raw = lax.all_gather(pieces, "rows", axis=1, tiled=True)

    region_ids = jnp.arange(region_count, dtype=jnp.int32)
    reads = jnp.logical_or(
        region_ids[None, :] == batch_owner[:, None],
        jnp.any(readers[:, :, None] == region_ids[None, None, :], axis=1),
    )
    table = jnp.concatenate(
        [obs_values[:, :, None], obs_error[:, :, None], jnp.swapaxes(loc_taper, 1, 2)], axis=2
    )
    picks = (obs_order[:, :, None] == jnp.arange(obs_count, dtype=jnp.int32)).astype(jnp.float32)
    slot_table = jnp.einsum("bsj,bjc->bsc", picks, table, precision=lax.Precision.HIGHEST)
    slot_values = slot_table[:, :, 0]
    slot_errors = slot_table[:, :, 1]
    slot_taper = jnp.swapaxes(slot_table[:, :, 2 : 2 + region_count], 1, 2)

    pending = [(raw, k) for k in range(batches)]
    scaled_list, incr_list = [], []
    for earlier in range(batches):
        source, index = pending[earlier]
        scaled, obs_incr = adjust_rows(source, index, slot_values[earlier], slot_errors[earlier])
        scaled_list.append(scaled)
        incr_list.append(obs_incr)
        for k in range(earlier + 1, batches):
            owner = batch_owner[k]
            source, index = pending[k]
            moved = lax.cond(
                reads[earlier, owner],
                lambda rows_x, s=scaled, o=obs_incr, w=slot_taper[earlier, owner], i=index: update_rows(
                    rows_x, i, [s], [o], w[None, None, None, :], jnp.ones((1,), jnp.int32),
                    obs_count, block=512,
                ),
                lambda rows_x, i=index: rows_x[i],
                source,
            )
            pending[k] = (moved[None], 0)

    main_weights = jnp.where(reads[:, region_idx, None], slot_taper[:, region_idx], 0.0)
    current = update_rows(
        ensemble_state[None], 0, scaled_list, incr_list, main_weights[None, :, None, :],
        reads[:, region_idx], ensemble_state.shape[0],
    )
    return current


def solution(mesh):
    placed = (P(("region", "rows"), None), P(), P(), P(), P(), P(), P(), P())
    return jax.shard_map(
        local, mesh=mesh, in_specs=placed, out_specs=P(("region", "rows"), None), check_vma=False
    )
```
